32 devices in a mesh: dp: 8 (over z, y), tensor: 4 (over x, core).
Axes of the slice: x: 2, y: 2, z: 4, core: 2. Of those that a mesh axis runs over, the one named last changes fastest.
Arguments:
- tokens: bfloat16 [16384, 1024], P(('dp', 'tensor')), may hold values from -6 to 6
- w_qkv: bfloat16 [3, 1024, 1024], P(None, None, 'tensor'), may hold values from -1 to 1
- w_out: bfloat16 [1024, 1024], P('tensor'), may hold values from -0.1875 to 0.1875
- w_up: bfloat16 [1024, 4096], P(None, 'tensor'), may hold values from -0.1875 to 0.1875
- w_down: bfloat16 [4096, 1024], P('tensor'), may hold values from -0.09375 to 0.09375
- key_pool: bfloat16 [1024, 128, 1024], P('dp', None, 'tensor'), may hold values from -16 to 16
- value_pool: bfloat16 [1024, 128, 1024], P('dp', None, 'tensor'), may hold values from -6 to 6
- prefix_keys: bfloat16 [128, 128, 1024], P('dp', None, 'tensor'), may hold values from -16 to 16
- prefix_values: bfloat16 [128, 128, 1024], P('dp', None, 'tensor'), may hold values from -15 to 15
- page_table: int32 [8, 128], P('dp'), may hold values from 0 to 127, each once within a row
- own_len: int32 [8, 8], P('dp'), may hold values from 1 to 2048, 10240 in all within a row
- group_of: int32 [8, 8], replicated, may hold values from 0 to 7
- prefix_table: int32 [128], replicated, may hold values from 0 to 127, each once
- prefix_len: int32 [8], replicated, may hold values from 1 to 2048, 10240 in all
- seg_ids: int32 [8, 2040], P('dp'), may hold values from 0 to 3, never falling along the last dimension, each value on 1 to 1020 neighbouring positions
Outputs:
- layer_out: bfloat16 [16384, 1024], P(('dp', 'tensor'))
The draws below stay inside these ranges and needn't reach their ends.
Inputs may be any that keep to these rules, and one draw needn't show every extreme that they name: `page_table`: each row lists every own page of the group once; decode request r uses entries r*16 to (r+1)*16 - 1. `prefix_table`: every prefix page once; prefix c uses entries c*16 to (c+1)*16 - 1; page p is stored by dp index p // 16. `seg_ids`: never falls along a row.
All inputs are finite; a program needn't handle non-finite values.
Results may differ from the reference program's by a relative error of at most 0.013.
Values may be sent and summed in bfloat16 or wider, within the bound.
No kernel may reach another device: no remote copies, remote signals or barrier semaphores. Data moves between devices by JAX's collectives and lax.ppermute only.
A program may use at most 192 MiB of HBM per device.

```python
import math
import jax
import jax.numpy as jnp
import numpy as np
from jax import lax

D = 1024
HEADS = 16
HDIM = 64
FF = 4096
PAGE = 128
TOK_GRP = 2048
DEC_DEV = 8
OWN_PAGES = 16
PRE_PAGES = 16
SEGS = 4
PRE = 2040
POOL = 128
PRE_POOL = 128
NGRP = 8
TOKENS = 16384
N_DP = 8
N_TENSOR = 4


def draw_tokens(key, part):
    noise_key = jax.random.fold_in(key, 11)
    return jnp.clip(jax.random.normal(noise_key, (TOKENS, D), jnp.float32), -6.0, 6.0).astype(jnp.bfloat16)


def draw_w_qkv(key, part):
    noise_key = jax.random.fold_in(key, 21)
    spread = 1.0 / math.sqrt(D)
    return (jnp.clip(jax.random.normal(noise_key, (3, D, D), jnp.float32), -6.0, 6.0) * spread).astype(jnp.bfloat16)


def cached_keys(key, pages, salt):
    noise_key = jax.random.fold_in(key, salt)
    return jnp.clip(2.5 * jax.random.normal(noise_key, (pages, PAGE, D), jnp.float32), -16.0, 16.0)


def draw_key_pool(key, part):
    return cached_keys(key, N_DP * POOL, 31).astype(jnp.bfloat16)


def draw_prefix_keys(key, part):
    return cached_keys(key, PRE_POOL, 41).astype(jnp.bfloat16)


def with_ends(array, key, least, largest):
    shape = array.shape
    spot = [jax.random.randint(jax.random.fold_in(key, axis), (), 0, shape[axis]) for axis in range(len(shape))]
    array = array.at[tuple(spot)].set(least)
    longest = shape.index(max(shape))
    spot[longest] = (spot[longest] + 1) % shape[longest]
    return array.at[tuple(spot)].set(largest)


def block_levels(rng, shape, cuts, least, high):
    level = 1.0
    for dim, shards_of in cuts:
        draws = jax.random.uniform(jax.random.fold_in(jax.random.fold_in(rng, 6), dim), (shards_of,), jnp.float32, least / len(cuts), high / len(cuts))
        level = level * jnp.repeat(jnp.exp(draws), shape[dim] // shards_of).reshape((-1,) + (1,) * (len(shape) - 1 - dim))
    return level


def length_profile(count, total, limit, lean):
    loads = [(1 << 20) // math.isqrt(grade ** lean) + 1 for grade in range(2, count + 1)]
    spare, holding = total - limit - (count - 1), [1] * (count - 1)
    while spare > 0:
        movable = [i for i in range(count - 1) if holding[i] < limit]
        pool, remaining = sum([loads[i] for i in movable]), spare
        for i in movable:
            addition = min(limit - holding[i], max(1, remaining * loads[i] // pool), spare)
            holding[i] = holding[i] + addition
            spare = spare - addition
    return np.array([limit] + holding)


def uneven_parts(stream_key, count, total, limit, skew):
    if count == 2:
        one = jax.random.randint(stream_key, (), max(1, total - limit), min(limit, total - 1) + 1)
        return jnp.stack([one, total - one])
    sizes = jnp.asarray(length_profile(count, total, limit, skew), jnp.int32)
    pairs = (count - 1) // 2
    giver, taker = sizes[1:1 + 2 * pairs:2], sizes[2:2 + 2 * pairs:2]
    slack = jnp.minimum(giver - 1, limit - taker)
    moved = jax.random.randint(jax.random.fold_in(stream_key, 1), (pairs,), 0, 1 << 20) % (slack + 1)
    sizes = sizes.at[1:1 + 2 * pairs:2].set(giver - moved).at[2:2 + 2 * pairs:2].set(taker + moved)
    return sizes[jax.random.permutation(jax.random.fold_in(stream_key, 2), count)]


def scatter_about(rng, extent, scale, bound, pieces=(), kind=jnp.bfloat16):
    factor_of = block_levels(rng, extent, pieces, -0.22, 0.18) if pieces else 1.0
    array = jax.random.normal(rng, extent, jnp.float32) * scale * factor_of
    return jnp.minimum(jnp.maximum(array, -bound), bound).astype(kind)


def setup_inputs(seed: int = 0) -> dict:
    key_list = jax.random.split(jax.random.key(seed), 16)
    tokens = draw_tokens(jax.random.fold_in(key_list[15], 71), 0)
    w_qkv = draw_w_qkv(jax.random.fold_in(key_list[15], 71), 0)
    w_out = scatter_about(key_list[2], (D, D), D ** -0.5, 0.1875, ((0, 4),))
    w_up = scatter_about(key_list[3], (D, FF), D ** -0.5, 0.1875, ((1, 4),))
    w_down = scatter_about(key_list[4], (FF, D), FF ** -0.5, 0.09375, ((0, 4),))
    key_pool = draw_key_pool(jax.random.fold_in(key_list[15], 71), 0)
    value_pool = scatter_about(key_list[6], (N_DP * POOL, PAGE, D), 1.0, 6.0, ((0, 8), (2, 4)))
    prefix_keys = draw_prefix_keys(jax.random.fold_in(key_list[15], 71), 0)
    prefix_values = scatter_about(key_list[8], (PRE_POOL, PAGE, D), 2.5, 15.0, ((0, 8), (2, 4)))
    page_table = jax.vmap(lambda own: jax.random.permutation(own, POOL))(jax.random.split(key_list[9], N_DP)).reshape((N_DP, POOL)).astype(jnp.int32)
    own_len = jax.vmap(lambda own: uneven_parts(own, DEC_DEV, DEC_DEV * OWN_PAGES * PAGE * 5 // 8, OWN_PAGES * PAGE, 2))(jax.random.split(key_list[10], N_DP)).reshape((N_DP, DEC_DEV)).astype(jnp.int32)
    group_of = with_ends(jax.random.randint(key_list[11], (N_DP, DEC_DEV), 0, NGRP), jax.random.fold_in(key_list[11], 1), 0, NGRP - 1).astype(jnp.int32)
    prefix_table = jax.random.permutation(key_list[12], PRE_POOL).astype(jnp.int32)
    prefix_len = uneven_parts(key_list[13], NGRP, NGRP * PRE_PAGES * PAGE * 5 // 8, PRE_PAGES * PAGE, 2).astype(jnp.int32)
    seg_ids = jax.vmap(lambda own: jnp.searchsorted(jnp.cumsum(uneven_parts(own, SEGS, PRE, PRE // 2, 2)), jnp.arange(PRE), side="right"))(jax.random.split(key_list[14], N_DP)).reshape((N_DP, PRE)).astype(jnp.int32)
    return dict(tokens=tokens, w_qkv=w_qkv, w_out=w_out, w_up=w_up, w_down=w_down, key_pool=key_pool, value_pool=value_pool, prefix_keys=prefix_keys, prefix_values=prefix_values, page_table=page_table, own_len=own_len, group_of=group_of, prefix_table=prefix_table, prefix_len=prefix_len, seg_ids=seg_ids)


negative_fill = -1e+30
epsilon = 1e-05

def rounded(matrix):
    return lax.optimization_barrier(matrix.astype(jnp.bfloat16))

def layer_norm(matrix):
    values = matrix.astype(jnp.float32)
    average = lax.optimization_barrier(jnp.mean(values, axis=-1, keepdims=True))
    centred = values - average
    variance = lax.optimization_barrier(jnp.mean(centred * centred, axis=-1, keepdims=True))
    return rounded(centred * lax.rsqrt(variance + epsilon))

def softmax_part(scores, visible, values, pattern):
    top = lax.optimization_barrier(jnp.max(jnp.where(visible, scores, negative_fill), axis=-1))
    weights = jnp.where(visible, jnp.exp(scores - top[..., None]), 0.0)
    total = lax.optimization_barrier(jnp.sum(weights, axis=-1))
    output = jnp.einsum(pattern, rounded(weights).astype(jnp.float32), values.astype(jnp.float32))
    return (top, total, output)

def combine_parts(first, second):
    top = jnp.maximum(first[0], second[0])
    scale_one = jnp.exp(first[0] - top)
    scale_two = jnp.exp(second[0] - top)
    return (top, first[1] * scale_one + second[1] * scale_two, first[2] * scale_one[..., None] + second[2] * scale_two[..., None])

def reference(tokens, w_qkv, w_out, w_up, w_down, key_pool, value_pool, prefix_keys, prefix_values, page_table, own_len, group_of, prefix_table, prefix_len, seg_ids):
    scale = 1.0 / math.sqrt(HDIM)
    prefill = TOK_GRP - DEC_DEV
    width = D // N_TENSOR
    hidden_width = FF // N_TENSOR
    block = min(512, TOK_GRP)

    def one_group(index):
        group_rows = lax.dynamic_slice_in_dim(tokens, index * TOK_GRP, TOK_GRP, 0)
        normed = layer_norm(group_rows)
        qkv = rounded(jnp.einsum('td,jde->jte', normed.astype(jnp.float32), w_qkv.astype(jnp.float32)))
        queries = qkv[0].reshape(TOK_GRP, HEADS, HDIM)
        keys = qkv[1].reshape(TOK_GRP, HEADS, HDIM)
        values = qkv[2].reshape(TOK_GRP, HEADS, HDIM)
        labels = jnp.concatenate([seg_ids[index], -1 - jnp.arange(DEC_DEV, dtype=jnp.int32)])
        positions = jnp.arange(TOK_GRP, dtype=jnp.int32)

        def batch_block(first):
            query_block = lax.dynamic_slice_in_dim(queries, first, block, 0)
            label_block = lax.dynamic_slice_in_dim(labels, first, block, 0)
            query_pos = first + jnp.arange(block, dtype=jnp.int32)
            scores = jnp.einsum('qhe,khe->hqk', query_block.astype(jnp.float32), keys.astype(jnp.float32)) * scale
            visible = (label_block[:, None] == labels[None, :]) & (positions[None, :] <= query_pos[:, None])
            part = softmax_part(scores, visible[None, :, :], values, 'hqk,khe->qhe')
            return (part[0].T, part[1].T, part[2])
        starts = jnp.arange(TOK_GRP // block, dtype=jnp.int32) * block
        top, total, output = lax.map(batch_block, starts)
        top = top.reshape(TOK_GRP, HEADS)
        total = total.reshape(TOK_GRP, HEADS)
        output = output.reshape(TOK_GRP, HEADS, HDIM)
        dec_queries = queries[prefill:].astype(jnp.float32)
        table = page_table[index].reshape(DEC_DEV, OWN_PAGES) + index * POOL
        own_keys = key_pool[table].reshape(DEC_DEV, OWN_PAGES * PAGE, HEADS, HDIM)
        own_values = value_pool[table].reshape(DEC_DEV, OWN_PAGES * PAGE, HEADS, HDIM)
        own_scores = jnp.einsum('dhe,dkhe->dhk', dec_queries, own_keys.astype(jnp.float32)) * scale
        own_visible = jnp.arange(OWN_PAGES * PAGE, dtype=jnp.int32)[None, :] < own_len[index][:, None]
        own_part = softmax_part(own_scores, own_visible[:, None, :], own_values, 'dhk,dkhe->dhe')
        groups = group_of[index]
        pre_table = prefix_table.reshape(NGRP, PRE_PAGES)[groups]
        pre_keys = prefix_keys[pre_table].reshape(DEC_DEV, PRE_PAGES * PAGE, HEADS, HDIM)
        pre_values = prefix_values[pre_table].reshape(DEC_DEV, PRE_PAGES * PAGE, HEADS, HDIM)
        pre_scores = jnp.einsum('dhe,dkhe->dhk', dec_queries, pre_keys.astype(jnp.float32)) * scale
        pre_visible = jnp.arange(PRE_PAGES * PAGE, dtype=jnp.int32)[None, :] < prefix_len[groups][:, None]
        pre_part = softmax_part(pre_scores, pre_visible[:, None, :], pre_values, 'dhk,dkhe->dhe')
        batch_dec = (top[prefill:], total[prefill:], output[prefill:])
        merged = combine_parts(combine_parts(batch_dec, own_part), pre_part)
        total = jnp.concatenate([total[:prefill], merged[1]], axis=0)
        output = jnp.concatenate([output[:prefill], merged[2]], axis=0)
        attention = rounded((output / total[..., None]).reshape(TOK_GRP, D))
        attn_sum = jnp.zeros((TOK_GRP, D), jnp.float32)
        for shard in range(N_TENSOR):
            term = jnp.dot(attention[:, shard * width:(shard + 1) * width], w_out[shard * width:(shard + 1) * width], preferred_element_type=jnp.float32)
            attn_sum = attn_sum + rounded(term).astype(jnp.float32)
        state = rounded(group_rows.astype(jnp.float32) + attn_sum)
        hidden = rounded(jax.nn.gelu(jnp.dot(layer_norm(state), w_up, preferred_element_type=jnp.float32), approximate=False))
        mlp_sum = jnp.zeros((TOK_GRP, D), jnp.float32)
        for shard in range(N_TENSOR):
            term = jnp.dot(hidden[:, shard * hidden_width:(shard + 1) * hidden_width], w_down[shard * hidden_width:(shard + 1) * hidden_width], preferred_element_type=jnp.float32)
            mlp_sum = mlp_sum + rounded(term).astype(jnp.float32)
        return (state.astype(jnp.float32) + mlp_sum).astype(jnp.bfloat16)
    outputs = lax.map(one_group, jnp.arange(N_DP, dtype=jnp.int32))
    return outputs.reshape(TOKENS, D)
```

```python
import jax
import jax.numpy as jnp
from jax import lax
from jax.sharding import PartitionSpec as P

HDIM = 64
SEG_MAX = 1020
Q_BLOCK = 256
K_ALIGN = 128


negative_fill = -1e30
epsilon = 1e-05


def layer_norm(matrix):
    values = matrix.astype(jnp.float32)
    average = jnp.mean(values, axis=-1, keepdims=True)
    centred = values - average
    variance = jnp.mean(centred * centred, axis=-1, keepdims=True)
    return (centred * lax.rsqrt(variance + epsilon)).astype(jnp.bfloat16)


def softmax_part(scores, visible, values, pattern):
    top = jnp.max(jnp.where(visible, scores, negative_fill), axis=-1)
    weights = jnp.where(visible, jnp.exp(scores - top[..., None]), 0.0)
    total = jnp.sum(weights, axis=-1)
    output = jnp.einsum(
        pattern, weights.astype(jnp.bfloat16), values, preferred_element_type=jnp.float32
    )
    return (top, total, output)


def combine_parts(first, second):
    top = jnp.maximum(first[0], second[0])
    scale_one = jnp.exp(first[0] - top)
    scale_two = jnp.exp(second[0] - top)
    return (
        top,
        first[1] * scale_one + second[1] * scale_two,
        first[2] * scale_one[..., None] + second[2] * scale_two[..., None],
    )


def block_rows(queries, heads):
    count, width = queries.shape
    rep = jnp.repeat(queries, heads, axis=0)
    row_head = jnp.arange(count * heads, dtype=jnp.int32) % heads
    col_head = jnp.arange(width, dtype=jnp.int32) // HDIM
    return jnp.where(row_head[:, None] == col_head[None, :], rep, jnp.zeros_like(rep))


def take_heads(output, count, heads):
    split = output.reshape(count, heads, heads, HDIM)
    eye = jnp.arange(heads)[:, None] == jnp.arange(heads)[None, :]
    return jnp.sum(jnp.where(eye[None, :, :, None], split, 0.0), axis=2)


def flat_part(query_rows, keys, values, visible, scale):
    scores = (
        lax.dot_general(
            query_rows, keys, (((1,), (1,)), ((), ())), preferred_element_type=jnp.float32
        )
        * scale
    )
    top = jnp.max(jnp.where(visible, scores, negative_fill), axis=-1)
    weights = jnp.where(visible, jnp.exp(scores - top[:, None]), 0.0)
    total = jnp.sum(weights, axis=-1)
    output = jnp.dot(weights.astype(jnp.bfloat16), values, preferred_element_type=jnp.float32)
    return top, total, output


def page_slots(table, page_ids):
    matches = table[:, None] == page_ids[None, :]
    index = jnp.arange(table.shape[0], dtype=jnp.int32)
    return jnp.sum(jnp.where(matches, index[:, None], 0), axis=0)


def per_device(
    tokens,
    w_qkv,
    w_out,
    w_up,
    w_down,
    key_pool,
    value_pool,
    prefix_keys,
    prefix_values,
    page_table,
    own_len,
    group_of,
    prefix_table,
    prefix_len,
    seg_ids,
):
    tensor_size = lax.axis_size("tensor")
    data_rank = lax.axis_index("dp")
    local_rows = tokens.shape[0]
    group_len = local_rows * tensor_size
    decodes = own_len.shape[1]
    prefill = group_len - decodes
    width = w_out.shape[0]
    heads_local = width // HDIM
    scale = HDIM ** (-0.5)
    qkv = jnp.einsum(
        "td,jde->jte",
        lax.all_gather(layer_norm(tokens), "tensor", axis=0, tiled=True),
        w_qkv,
        preferred_element_type=jnp.float32,
    ).astype(jnp.bfloat16)
    queries = qkv[0]
    keys = qkv[1]
    values = qkv[2]
    labels = jnp.concatenate([seg_ids[0], -1 - jnp.arange(decodes, dtype=jnp.int32)])

    block = min(Q_BLOCK, group_len)
    tops, totals, outs = [], [], []
    for first in range(0, group_len, block):
        low = max(0, ((first - (SEG_MAX - 1)) // K_ALIGN) * K_ALIGN)
        high = first + block
        span = high - low
        query_block = queries[first:high].reshape(block, heads_local, HDIM)
        key_block = keys[low:high].reshape(span, heads_local, HDIM)
        value_block = values[low:high].reshape(span, heads_local, HDIM)
        scores = (
            jnp.einsum("qhe,khe->hqk", query_block, key_block, preferred_element_type=jnp.float32)
            * scale
        )
        query_pos = jnp.arange(first, high, dtype=jnp.int32)
        key_pos = jnp.arange(low, high, dtype=jnp.int32)
        visible = (labels[first:high][:, None] == labels[low:high][None, :]) & (
            key_pos[None, :] <= query_pos[:, None]
        )
        part = softmax_part(scores, visible[None, :, :], value_block, "hqk,khe->qhe")
        tops.append(part[0].T)
        totals.append(part[1].T)
        outs.append(part[2])
    top = jnp.concatenate(tops, axis=0)
    total = jnp.concatenate(totals, axis=0)
    output = jnp.concatenate(outs, axis=0)

    dec_queries = queries[prefill:]
    rows_h = decodes * heads_local
    row_req = jnp.arange(rows_h, dtype=jnp.int32) // heads_local

    pages, page_len = key_pool.shape[0], key_pool.shape[1]
    table = page_table[0]
    own_pages = table.shape[0] // decodes
    slot = page_slots(table, jnp.arange(pages, dtype=jnp.int32))
    owner = jnp.repeat(slot // own_pages, page_len)
    offset = ((slot % own_pages)[:, None] * page_len + jnp.arange(page_len)[None, :]).reshape(-1)
    own_visible = (owner[None, :] == row_req[:, None]) & (
        offset[None, :] < own_len[0][row_req][:, None]
    )
    o_top, o_total, o_out = flat_part(
        block_rows(dec_queries, heads_local),
        key_pool.reshape(pages * page_len, width),
        value_pool.reshape(pages * page_len, width),
        own_visible,
        scale,
    )
    own_part = (
        o_top.reshape(decodes, heads_local),
        o_total.reshape(decodes, heads_local),
        take_heads(o_out, decodes, heads_local),
    )

    all_queries = lax.all_gather(dec_queries, "dp", axis=0, tiled=True)
    all_count = all_queries.shape[0]
    all_rows = all_count * heads_local
    pre_local = prefix_keys.shape[0]
    per_prefix = prefix_table.shape[0] // prefix_len.shape[0]
    page_ids = data_rank * pre_local + jnp.arange(pre_local, dtype=jnp.int32)
    pslot = page_slots(prefix_table, page_ids)
    p_owner = jnp.repeat(pslot // per_prefix, page_len)
    p_offset = (
        (pslot % per_prefix)[:, None] * page_len + jnp.arange(page_len)[None, :]
    ).reshape(-1)
    row_prefix = group_of.reshape(-1)[jnp.arange(all_rows, dtype=jnp.int32) // heads_local]
    p_visible = (p_owner[None, :] == row_prefix[:, None]) & (
        p_offset[None, :] < prefix_len[row_prefix][:, None]
    )
    p_top, p_total, p_out = flat_part(
        block_rows(all_queries, heads_local),
        prefix_keys.reshape(pre_local * page_len, width),
        prefix_values.reshape(pre_local * page_len, width),
        p_visible,
        scale,
    )
    packed = jnp.concatenate(
        [
            take_heads(p_out, all_count, heads_local),
            p_top.reshape(all_count, heads_local, 1),
            p_total.reshape(all_count, heads_local, 1),
        ],
        axis=-1,
    )
    gathered = lax.all_gather(packed, "dp", axis=0, tiled=False)
    mine = lax.dynamic_slice_in_dim(gathered, data_rank * decodes, decodes, axis=1)
    m_all = mine[..., HDIM]
    p_max = jnp.max(m_all, axis=0)
    p_scale = jnp.exp(m_all - p_max[None])
    prefix_result = (
        p_max,
        jnp.sum(mine[..., HDIM + 1] * p_scale, axis=0),
        jnp.sum(mine[..., :HDIM] * p_scale[..., None], axis=0),
    )

    batch_dec = (top[prefill:], total[prefill:], output[prefill:])
    merged_dec = combine_parts(combine_parts(batch_dec, own_part), prefix_result)
    total = jnp.concatenate([total[:prefill], merged_dec[1]], axis=0)
    output = jnp.concatenate([output[:prefill], merged_dec[2]], axis=0)
    attention = (output / total[..., None]).reshape(group_len, width).astype(jnp.bfloat16)
    attn_share = lax.psum_scatter(
        jnp.dot(attention, w_out, preferred_element_type=jnp.float32).astype(jnp.bfloat16),
        "tensor",
        scatter_dimension=0,
        tiled=True,
    ).astype(jnp.float32)
    state = (tokens.astype(jnp.float32) + attn_share).astype(jnp.bfloat16)
    hidden = jax.nn.gelu(
        jnp.dot(
            lax.all_gather(layer_norm(state), "tensor", axis=0, tiled=True),
            w_up,
            preferred_element_type=jnp.float32,
        ),
        approximate=False,
    ).astype(jnp.bfloat16)
    mlp_share = lax.psum_scatter(
        jnp.dot(hidden, w_down, preferred_element_type=jnp.float32).astype(jnp.bfloat16),
        "tensor",
        scatter_dimension=0,
        tiled=True,
    ).astype(jnp.float32)
    return (state.astype(jnp.float32) + mlp_share).astype(jnp.bfloat16)


def solution(mesh):
    placed = (
        P(("dp", "tensor"), None),
        P(None, None, "tensor"),
        P("tensor", None),
        P(None, "tensor"),
        P("tensor", None),
        P("dp", None, "tensor"),
        P("dp", None, "tensor"),
        P("dp", None, "tensor"),
        P("dp", None, "tensor"),
        P("dp", None),
        P("dp", None),
        P(),
        P(),
        P(),
        P("dp", None),
    )
    return jax.shard_map(
        per_device, mesh=mesh, in_specs=placed, out_specs=P(("dp", "tensor"), None), check_vma=False
    )
```

```python
import jax
import jax.numpy as jnp
from jax import lax
from jax.sharding import PartitionSpec as P

HDIM = 64
SEG_MAX = 1020
Q_BLOCK = 256
K_ALIGN = 128


negative_fill = -1e30
epsilon = 1e-05


def layer_norm(matrix):
    values = matrix.astype(jnp.float32)
    average = jnp.mean(values, axis=-1, keepdims=True)
    centred = values - average
    variance = jnp.mean(centred * centred, axis=-1, keepdims=True)
    return (centred * lax.rsqrt(variance + epsilon)).astype(jnp.bfloat16)


def softmax_part(scores, visible, values, pattern):
    top = jnp.max(jnp.where(visible, scores, negative_fill), axis=-1)
    weights = jnp.where(visible, jnp.exp(scores - top[..., None]), 0.0)
    total = jnp.sum(weights, axis=-1)
    output = jnp.einsum(
        pattern, weights.astype(jnp.bfloat16), values, preferred_element_type=jnp.float32
    )
    return (top, total, output)


def combine_parts(first, second):
    top = jnp.maximum(first[0], second[0])
    scale_one = jnp.exp(first[0] - top)
    scale_two = jnp.exp(second[0] - top)
    return (
        top,
        first[1] * scale_one + second[1] * scale_two,
        first[2] * scale_one[..., None] + second[2] * scale_two[..., None],
    )


def block_rows(queries, heads):
    count, width = queries.shape
    rep = jnp.repeat(queries, heads, axis=0)
    row_head = jnp.arange(count * heads, dtype=jnp.int32) % heads
    col_head = jnp.arange(width, dtype=jnp.int32) // HDIM
    return jnp.where(row_head[:, None] == col_head[None, :], rep, jnp.zeros_like(rep))


def take_heads(output, count, heads):
    split = output.reshape(count, heads, heads, HDIM)
    eye = jnp.arange(heads)[:, None] == jnp.arange(heads)[None, :]
    return jnp.sum(jnp.where(eye[None, :, :, None], split, 0.0), axis=2)


def flat_part(query_rows, keys, values, visible, scale):
    scores = (
        lax.dot_general(
            query_rows, keys, (((1,), (1,)), ((), ())), preferred_element_type=jnp.float32
        )
        * scale
    )
    top = jnp.max(jnp.where(visible, scores, negative_fill), axis=-1)
    weights = jnp.where(visible, jnp.exp(scores - top[:, None]), 0.0)
    total = jnp.sum(weights, axis=-1)
    output = jnp.dot(weights.astype(jnp.bfloat16), values, preferred_element_type=jnp.float32)
    return top, total, output


def page_slots(table, page_ids):
    matches = table[:, None] == page_ids[None, :]
    index = jnp.arange(table.shape[0], dtype=jnp.int32)
    return jnp.sum(jnp.where(matches, index[:, None], 0), axis=0)


def per_device(
    tokens,
    w_qkv,
    w_out,
    w_up,
    w_down,
    key_pool,
    value_pool,
    prefix_keys,
    prefix_values,
    page_table,
    own_len,
    group_of,
    prefix_table,
    prefix_len,
    seg_ids,
):
    tensor_size = lax.axis_size("tensor")
    data_rank = lax.axis_index("dp")
    local_rows = tokens.shape[0]
    group_len = local_rows * tensor_size
    decodes = own_len.shape[1]
    prefill = group_len - decodes
    width = w_out.shape[0]
    heads_local = width // HDIM
    scale = HDIM ** (-0.5)
    qkv = jnp.einsum(
        "td,jde->jte",
        lax.all_gather(layer_norm(tokens), "tensor", axis=0, tiled=True),
        w_qkv,
        preferred_element_type=jnp.float32,
    ).astype(jnp.bfloat16)
    queries = qkv[0]
    keys = qkv[1]
    values = qkv[2]
    labels = jnp.concatenate([seg_ids[0], -1 - jnp.arange(decodes, dtype=jnp.int32)])

    block = min(Q_BLOCK, group_len)
    tops, totals, outs = [], [], []
    for first in range(0, group_len, block):
        low = max(0, ((first - (SEG_MAX - 1)) // K_ALIGN) * K_ALIGN)
        high = first + block
        span = high - low
        query_block = queries[first:high].reshape(block, heads_local, HDIM)
        key_block = keys[low:high].reshape(span, heads_local, HDIM)
        value_block = values[low:high].reshape(span, heads_local, HDIM)
        scores = (
            jnp.einsum("qhe,khe->hqk", query_block, key_block, preferred_element_type=jnp.float32)
            * scale
        )
        query_pos = jnp.arange(first, high, dtype=jnp.int32)
        key_pos = jnp.arange(low, high, dtype=jnp.int32)
        visible = (labels[first:high][:, None] == labels[low:high][None, :]) & (
            key_pos[None, :] <= query_pos[:, None]
        )
        part = softmax_part(scores, visible[None, :, :], value_block, "hqk,khe->qhe")
        tops.append(part[0].T)
        totals.append(part[1].T)
        outs.append(part[2])
    top = jnp.concatenate(tops, axis=0)
    total = jnp.concatenate(totals, axis=0)
    output = jnp.concatenate(outs, axis=0)

    dec_queries = queries[prefill:]
    rows_h = decodes * heads_local
    row_req = jnp.arange(rows_h, dtype=jnp.int32) // heads_local

    pages, page_len = key_pool.shape[0], key_pool.shape[1]
    table = page_table[0]
    own_pages = table.shape[0] // decodes
    slot = page_slots(table, jnp.arange(pages, dtype=jnp.int32))
    owner = jnp.repeat(slot // own_pages, page_len)
    offset = ((slot % own_pages)[:, None] * page_len + jnp.arange(page_len)[None, :]).reshape(-1)
    own_visible = (owner[None, :] == row_req[:, None]) & (
        offset[None, :] < own_len[0][row_req][:, None]
    )
    o_top, o_total, o_out = flat_part(
        block_rows(dec_queries, heads_local),
        key_pool.reshape(pages * page_len, width),
        value_pool.reshape(pages * page_len, width),
        own_visible,
        scale,
    )
    own_part = (
        o_top.reshape(decodes, heads_local),
        o_total.reshape(decodes, heads_local),
        take_heads(o_out, decodes, heads_local),
    )

    data_size = lax.axis_size("dp")
    shifted = [dec_queries] + [
        lax.ppermute(dec_queries, "dp", [(i, (i + k) % data_size) for i in range(data_size)])
        for k in range(1, data_size)
    ]
    source_order = (data_rank - jnp.arange(data_size, dtype=jnp.int32)) % data_size
    all_queries = jnp.take(jnp.stack(shifted), source_order, axis=0).reshape(
        data_size * decodes, width
    )
    all_count = all_queries.shape[0]
    all_rows = all_count * heads_local
    pre_local = prefix_keys.shape[0]
    per_prefix = prefix_table.shape[0] // prefix_len.shape[0]
    page_ids = data_rank * pre_local + jnp.arange(pre_local, dtype=jnp.int32)
    pslot = page_slots(prefix_table, page_ids)
    p_owner = jnp.repeat(pslot // per_prefix, page_len)
    p_offset = (
        (pslot % per_prefix)[:, None] * page_len + jnp.arange(page_len)[None, :]
    ).reshape(-1)
    row_prefix = group_of.reshape(-1)[jnp.arange(all_rows, dtype=jnp.int32) // heads_local]
    p_visible = (p_owner[None, :] == row_prefix[:, None]) & (
        p_offset[None, :] < prefix_len[row_prefix][:, None]
    )
    p_top, p_total, p_out = flat_part(
        block_rows(all_queries, heads_local),
        prefix_keys.reshape(pre_local * page_len, width),
        prefix_values.reshape(pre_local * page_len, width),
        p_visible,
        scale,
    )
    packed = jnp.concatenate(
        [
            take_heads(p_out, all_count, heads_local),
            p_top.reshape(all_count, heads_local, 1),
            p_total.reshape(all_count, heads_local, 1),
        ],
        axis=-1,
    )
    received = [lax.dynamic_slice_in_dim(packed, data_rank * decodes, decodes, axis=0)]
    for k in range(1, data_size):
        target = (data_rank + k) % data_size
        outgoing = lax.dynamic_slice_in_dim(packed, target * decodes, decodes, axis=0)
        received.append(
            lax.ppermute(outgoing, "dp", [(i, (i + k) % data_size) for i in range(data_size)])
        )
    mine = jnp.stack(received)
    m_all = mine[..., HDIM]
    p_max = jnp.max(m_all, axis=0)
    p_scale = jnp.exp(m_all - p_max[None])
    prefix_result = (
        p_max,
        jnp.sum(mine[..., HDIM + 1] * p_scale, axis=0),
        jnp.sum(mine[..., :HDIM] * p_scale[..., None], axis=0),
    )

    batch_dec = (top[prefill:], total[prefill:], output[prefill:])
    merged_dec = combine_parts(combine_parts(batch_dec, own_part), prefix_result)
    total = jnp.concatenate([total[:prefill], merged_dec[1]], axis=0)
    output = jnp.concatenate([output[:prefill], merged_dec[2]], axis=0)
    attention = (output / total[..., None]).reshape(group_len, width).astype(jnp.bfloat16)
    attn_share = lax.psum_scatter(
        jnp.dot(attention, w_out, preferred_element_type=jnp.float32).astype(jnp.bfloat16),
        "tensor",
        scatter_dimension=0,
        tiled=True,
    ).astype(jnp.float32)
    state = (tokens.astype(jnp.float32) + attn_share).astype(jnp.bfloat16)
    hidden = jax.nn.gelu(
        jnp.dot(
            lax.all_gather(layer_norm(state), "tensor", axis=0, tiled=True),
            w_up,
            preferred_element_type=jnp.float32,
        ),
        approximate=False,
    ).astype(jnp.bfloat16)
    mlp_share = lax.psum_scatter(
        jnp.dot(hidden, w_down, preferred_element_type=jnp.float32).astype(jnp.bfloat16),
        "tensor",
        scatter_dimension=0,
        tiled=True,
    ).astype(jnp.float32)
    return (state.astype(jnp.float32) + mlp_share).astype(jnp.bfloat16)


def solution(mesh):
    placed = (
        P(("dp", "tensor"), None),
        P(None, None, "tensor"),
        P("tensor", None),
        P(None, "tensor"),
        P("tensor", None),
        P("dp", None, "tensor"),
        P("dp", None, "tensor"),
        P("dp", None, "tensor"),
        P("dp", None, "tensor"),
        P("dp", None),
        P("dp", None),
        P(),
        P(),
        P(),
        P("dp", None),
    )
    return jax.shard_map(
        per_device, mesh=mesh, in_specs=placed, out_specs=P(("dp", "tensor"), None), check_vma=False
    )
```

```python
import jax
import jax.numpy as jnp
from jax import lax
from jax.sharding import Mesh, PartitionSpec as P

HDIM = 64
SEG_MAX = 1020
Q_BLOCK = 256
K_ALIGN = 128


negative_fill = -1e30
epsilon = 1e-05


def layer_norm(matrix):
    values = matrix.astype(jnp.float32)
    average = jnp.mean(values, axis=-1, keepdims=True)
    centred = values - average
    variance = jnp.mean(centred * centred, axis=-1, keepdims=True)
    return (centred * lax.rsqrt(variance + epsilon)).astype(jnp.bfloat16)


def softmax_part(scores, visible, values, pattern):
    top = jnp.max(jnp.where(visible, scores, negative_fill), axis=-1)
    weights = jnp.where(visible, jnp.exp(scores - top[..., None]), 0.0)
    total = jnp.sum(weights, axis=-1)
    output = jnp.einsum(
        pattern, weights.astype(jnp.bfloat16), values, preferred_element_type=jnp.float32
    )
    return (top, total, output)


def combine_parts(first, second):
    top = jnp.maximum(first[0], second[0])
    scale_one = jnp.exp(first[0] - top)
    scale_two = jnp.exp(second[0] - top)
    return (
        top,
        first[1] * scale_one + second[1] * scale_two,
        first[2] * scale_one[..., None] + second[2] * scale_two[..., None],
    )


def block_rows(queries, heads):
    count, width = queries.shape
    rep = jnp.repeat(queries, heads, axis=0)
    row_head = jnp.arange(count * heads, dtype=jnp.int32) % heads
    col_head = jnp.arange(width, dtype=jnp.int32) // HDIM
    return jnp.where(row_head[:, None] == col_head[None, :], rep, jnp.zeros_like(rep))


def take_heads(output, count, heads):
    split = output.reshape(count, heads, heads, HDIM)
    eye = jnp.arange(heads)[:, None] == jnp.arange(heads)[None, :]
    return jnp.sum(jnp.where(eye[None, :, :, None], split, 0.0), axis=2)


def flat_part(query_rows, keys, values, visible, scale):
    scores = (
        lax.dot_general(
            keys, query_rows, (((1,), (1,)), ((), ())), preferred_element_type=jnp.float32
        )
        * scale
    )
    top = jnp.max(jnp.where(visible, scores, negative_fill), axis=0)
    weights = jnp.where(visible, jnp.exp(scores - top[None, :]), 0.0)
    total = jnp.sum(weights, axis=0)
    output = lax.dot_general(
        weights.astype(jnp.bfloat16),
        values,
        (((0,), (0,)), ((), ())),
        preferred_element_type=jnp.float32,
    )
    return top, total, output


def page_slots(table, page_ids):
    matches = table[:, None] == page_ids[None, :]
    index = jnp.arange(table.shape[0], dtype=jnp.int32)
    return jnp.sum(jnp.where(matches, index[:, None], 0), axis=0)


def per_device(
    tokens,
    w_qkv,
    w_out,
    w_up,
    w_down,
    key_pool,
    value_pool,
    prefix_keys,
    prefix_values,
    page_table,
    own_len,
    group_of,
    prefix_table,
    prefix_len,
    seg_ids,
):
    chips = lax.axis_size("tx")
    cores = lax.axis_size("tc")
    tensor_size = chips * cores
    data_rank = lax.axis_index("dp")
    local_rows = tokens.shape[0]
    group_len = local_rows * tensor_size
    decodes = own_len.shape[1]
    prefill = group_len - decodes
    width = w_out.shape[0]
    heads_local = width // HDIM
    scale = HDIM ** (-0.5)
    gathered = lax.all_gather(
        lax.all_gather(layer_norm(tokens), "tx", axis=0, tiled=False), "tc", axis=0, tiled=False
    )
    normed = jnp.swapaxes(gathered, 0, 1).reshape(group_len, tokens.shape[1])
    qkv = jnp.einsum(
        "td,jde->jte", normed, w_qkv, preferred_element_type=jnp.float32
    ).astype(jnp.bfloat16)
    queries = qkv[0]
    keys = qkv[1]
    values = qkv[2]
    labels = jnp.concatenate([seg_ids[0], -1 - jnp.arange(decodes, dtype=jnp.int32)])

    block = min(Q_BLOCK, group_len)
    tops, totals, outs = [], [], []
    for first in range(0, group_len, block):
        low = max(0, ((first - (SEG_MAX - 1)) // K_ALIGN) * K_ALIGN)
        high = first + block
        span = high - low
        query_block = queries[first:high].reshape(block, heads_local, HDIM)
        key_block = keys[low:high].reshape(span, heads_local, HDIM)
        value_block = values[low:high].reshape(span, heads_local, HDIM)
        scores = (
            jnp.einsum("qhe,khe->hqk", query_block, key_block, preferred_element_type=jnp.float32)
            * scale
        )
        query_pos = jnp.arange(first, high, dtype=jnp.int32)
        key_pos = jnp.arange(low, high, dtype=jnp.int32)
        visible = (labels[first:high][:, None] == labels[low:high][None, :]) & (
            key_pos[None, :] <= query_pos[:, None]
        )
        part = softmax_part(scores, visible[None, :, :], value_block, "hqk,khe->qhe")
        tops.append(part[0].T)
        totals.append(part[1].T)
        outs.append(part[2])
    top = jnp.concatenate(tops, axis=0)
    total = jnp.concatenate(totals, axis=0)
    output = jnp.concatenate(outs, axis=0)

    dec_queries = queries[prefill:]
    rows_h = decodes * heads_local
    row_req = jnp.arange(rows_h, dtype=jnp.int32) // heads_local

    pages, page_len = key_pool.shape[0], key_pool.shape[1]
    table = page_table[0]
    own_pages = table.shape[0] // decodes
    slot = page_slots(table, jnp.arange(pages, dtype=jnp.int32))
    owner = jnp.repeat(slot // own_pages, page_len)
    offset = ((slot % own_pages)[:, None] * page_len + jnp.arange(page_len)[None, :]).reshape(-1)
    own_visible = (owner[:, None] == row_req[None, :]) & (
        offset[:, None] < own_len[0][row_req][None, :]
    )
    o_top, o_total, o_out = flat_part(
        block_rows(dec_queries, heads_local),
        key_pool.reshape(pages * page_len, width),
        value_pool.reshape(pages * page_len, width),
        own_visible,
        scale,
    )
    own_part = (
        o_top.reshape(decodes, heads_local),
        o_total.reshape(decodes, heads_local),
        take_heads(o_out, decodes, heads_local),
    )

    data_size = lax.axis_size("dp")
    shifted = [dec_queries] + [
        lax.ppermute(dec_queries, "dp", [(i, (i + k) % data_size) for i in range(data_size)])
        for k in range(1, data_size)
    ]
    source_order = (data_rank - jnp.arange(data_size, dtype=jnp.int32)) % data_size
    all_queries = jnp.take(jnp.stack(shifted), source_order, axis=0).reshape(
        data_size * decodes, width
    )
    all_count = all_queries.shape[0]
    all_rows = all_count * heads_local
    pre_local = prefix_keys.shape[0]
    per_prefix = prefix_table.shape[0] // prefix_len.shape[0]
    page_ids = data_rank * pre_local + jnp.arange(pre_local, dtype=jnp.int32)
    pslot = page_slots(prefix_table, page_ids)
    p_owner = jnp.repeat(pslot // per_prefix, page_len)
    p_offset = (
        (pslot % per_prefix)[:, None] * page_len + jnp.arange(page_len)[None, :]
    ).reshape(-1)
    row_prefix = group_of.reshape(-1)[jnp.arange(all_rows, dtype=jnp.int32) // heads_local]
    p_visible = (p_owner[:, None] == row_prefix[None, :]) & (
        p_offset[:, None] < prefix_len[row_prefix][None, :]
    )
    p_top, p_total, p_out = flat_part(
        block_rows(all_queries, heads_local),
        prefix_keys.reshape(pre_local * page_len, width),
        prefix_values.reshape(pre_local * page_len, width),
        p_visible,
        scale,
    )
    packed = jnp.concatenate(
        [
            take_heads(p_out, all_count, heads_local),
            p_top.reshape(all_count, heads_local, 1),
            p_total.reshape(all_count, heads_local, 1),
        ],
        axis=-1,
    )
    received = [lax.dynamic_slice_in_dim(packed, data_rank * decodes, decodes, axis=0)]
    for k in range(1, data_size):
        target = (data_rank + k) % data_size
        outgoing = lax.dynamic_slice_in_dim(packed, target * decodes, decodes, axis=0)
        received.append(
            lax.ppermute(outgoing, "dp", [(i, (i + k) % data_size) for i in range(data_size)])
        )
    mine = jnp.stack(received)
    m_all = mine[..., HDIM]
    p_max = jnp.max(m_all, axis=0)
    p_scale = jnp.exp(m_all - p_max[None])
    prefix_result = (
        p_max,
        jnp.sum(mine[..., HDIM + 1] * p_scale, axis=0),
        jnp.sum(mine[..., :HDIM] * p_scale[..., None], axis=0),
    )

    batch_dec = (top[prefill:], total[prefill:], output[prefill:])
    merged_dec = combine_parts(combine_parts(batch_dec, own_part), prefix_result)
    total = jnp.concatenate([total[:prefill], merged_dec[1]], axis=0)
    output = jnp.concatenate([output[:prefill], merged_dec[2]], axis=0)
    attention = (output / total[..., None]).reshape(group_len, width).astype(jnp.bfloat16)
    projected = jnp.dot(attention, w_out, preferred_element_type=jnp.float32).astype(jnp.bfloat16)
    projected = jnp.swapaxes(projected.reshape(chips, cores, local_rows, -1), 0, 1)
    attn_share = lax.psum_scatter(
        lax.psum_scatter(projected, "tc", scatter_dimension=0, tiled=False),
        "tx",
        scatter_dimension=0,
        tiled=False,
    ).astype(jnp.float32)
    state = (tokens.astype(jnp.float32) + attn_share).astype(jnp.bfloat16)
    state_rows = lax.all_gather(
        lax.all_gather(layer_norm(state), "tx", axis=0, tiled=False), "tc", axis=0, tiled=False
    ).reshape(group_len, -1)
    hidden = jax.nn.gelu(
        jnp.dot(state_rows, w_up, preferred_element_type=jnp.float32), approximate=False
    ).astype(jnp.bfloat16)
    mlp_part = jnp.dot(hidden, w_down, preferred_element_type=jnp.float32).astype(jnp.bfloat16)
    mlp_share = lax.psum_scatter(
        lax.psum_scatter(
            mlp_part.reshape(cores, chips, local_rows, -1), "tc", scatter_dimension=0, tiled=False
        ),
        "tx",
        scatter_dimension=0,
        tiled=False,
    ).astype(jnp.float32)
    return (state.astype(jnp.float32) + mlp_share).astype(jnp.bfloat16)


def solution(mesh):
    data_size = mesh.shape["dp"]
    tensor_size = mesh.shape["tensor"]
    split = Mesh(mesh.devices.reshape(data_size, tensor_size // 2, 2), ("dp", "tx", "tc"))
    placed = (
        P(("dp", "tx", "tc"), None),
        P(None, None, ("tx", "tc")),
        P(("tx", "tc"), None),
        P(None, ("tx", "tc")),
        P(("tx", "tc"), None),
        P("dp", None, ("tx", "tc")),
        P("dp", None, ("tx", "tc")),
        P("dp", None, ("tx", "tc")),
        P("dp", None, ("tx", "tc")),
        P("dp", None),
        P("dp", None),
        P(),
        P(),
        P(),
        P("dp", None),
    )
    return jax.shard_map(
        per_device, mesh=split, in_specs=placed, out_specs=P(("dp", "tx", "tc"), None), check_vma=False
    )
```

```python
import jax
import jax.numpy as jnp
from jax import lax
from jax.sharding import Mesh, PartitionSpec as P

HDIM = 64
SEG_MAX = 1020
Q_BLOCK = 256
K_ALIGN = 128


negative_fill = -1e30
epsilon = 1e-05


def layer_norm(matrix):
    values = matrix.astype(jnp.float32)
    average = jnp.mean(values, axis=-1, keepdims=True)
    centred = values - average
    variance = jnp.mean(centred * centred, axis=-1, keepdims=True)
    return (centred * lax.rsqrt(variance + epsilon)).astype(jnp.bfloat16)


def softmax_part(scores, visible, values, pattern):
    top = jnp.max(jnp.where(visible, scores, negative_fill), axis=-1)
    weights = jnp.where(visible, jnp.exp(scores - top[..., None]), 0.0)
    total = jnp.sum(weights, axis=-1)
    output = jnp.einsum(
        pattern, weights.astype(jnp.bfloat16), values, preferred_element_type=jnp.float32
    )
    return (top, total, output)


def combine_parts(first, second):
    top = jnp.maximum(first[0], second[0])
    scale_one = jnp.exp(first[0] - top)
    scale_two = jnp.exp(second[0] - top)
    return (
        top,
        first[1] * scale_one + second[1] * scale_two,
        first[2] * scale_one[..., None] + second[2] * scale_two[..., None],
    )


def block_rows(queries, heads):
    count, width = queries.shape
    rep = jnp.repeat(queries, heads, axis=0)
    row_head = jnp.arange(count * heads, dtype=jnp.int32) % heads
    col_head = jnp.arange(width, dtype=jnp.int32) // HDIM
    return jnp.where(row_head[:, None] == col_head[None, :], rep, jnp.zeros_like(rep))


def take_heads(output, count, heads):
    split = output.reshape(count, heads, heads, HDIM)
    eye = jnp.arange(heads)[:, None] == jnp.arange(heads)[None, :]
    return jnp.sum(jnp.where(eye[None, :, :, None], split, 0.0), axis=2)


def flat_part(query_rows, keys, values, visible, scale):
    scores = (
        lax.dot_general(
            keys, query_rows, (((1,), (1,)), ((), ())), preferred_element_type=jnp.float32
        )
        * scale
    )
    top = jnp.max(jnp.where(visible, scores, negative_fill), axis=0)
    weights = jnp.where(visible, jnp.exp(scores - top[None, :]), 0.0)
    total = jnp.sum(weights, axis=0)
    output = jnp.dot(weights.T.astype(jnp.bfloat16), values, preferred_element_type=jnp.float32)
    return top, total, output


def page_slots(table, page_ids):
    matches = table[:, None] == page_ids[None, :]
    index = jnp.arange(table.shape[0], dtype=jnp.int32)
    return jnp.sum(jnp.where(matches, index[:, None], 0), axis=0)


def ring(axis, shift):
    size = lax.axis_size(axis)
    return [(i, (i + shift) % size) for i in range(size)]


def gather_rows(rows):
    chips = lax.axis_size("tx")
    chip = lax.axis_index("tx")
    core = lax.axis_index("tc")
    pieces = [rows] + [lax.ppermute(rows, "tx", ring("tx", k)) for k in range(1, chips)]
    order = (chip - jnp.arange(chips, dtype=jnp.int32)) % chips
    held = jnp.take(jnp.stack(pieces), order, axis=0)
    other = lax.ppermute(held, "tc", ring("tc", 1))
    pair = jnp.where(core == 0, jnp.stack([held, other], 1), jnp.stack([other, held], 1))
    return pair.reshape(-1, rows.shape[1])


def scatter_sum(partial):
    chips = lax.axis_size("tx")
    chip = lax.axis_index("tx")
    core = lax.axis_index("tc")
    split = partial.reshape(chips, 2, -1, partial.shape[1])
    keep = lax.dynamic_index_in_dim(split, core, 1, keepdims=False)
    send = lax.dynamic_index_in_dim(split, 1 - core, 1, keepdims=False)
    chip_sum = keep.astype(jnp.float32) + lax.ppermute(send, "tc", ring("tc", 1)).astype(
        jnp.float32
    )
    chip_half = chip_sum.astype(jnp.bfloat16)
    total = lax.dynamic_index_in_dim(chip_sum, chip, 0, keepdims=False)
    for k in range(1, chips):
        outgoing = lax.dynamic_index_in_dim(chip_half, (chip + k) % chips, 0, keepdims=False)
        total = total + lax.ppermute(outgoing, "tx", ring("tx", k)).astype(jnp.float32)
    return total


def per_device(
    tokens,
    w_qkv,
    w_out,
    w_up,
    w_down,
    key_pool,
    value_pool,
    prefix_keys,
    prefix_values,
    page_table,
    own_len,
    group_of,
    prefix_table,
    prefix_len,
    seg_ids,
):
    chips = lax.axis_size("tx")
    cores = lax.axis_size("tc")
    tensor_size = chips * cores
    data_rank = lax.axis_index("dp")
    local_rows = tokens.shape[0]
    group_len = local_rows * tensor_size
    decodes = own_len.shape[1]
    prefill = group_len - decodes
    width = w_out.shape[0]
    heads_local = width // HDIM
    scale = HDIM ** (-0.5)
    normed = gather_rows(layer_norm(tokens))
    qkv = jnp.einsum(
        "td,jde->jte", normed, w_qkv, preferred_element_type=jnp.float32
    ).astype(jnp.bfloat16)
    queries = qkv[0]
    keys = qkv[1]
    values = qkv[2]
    labels = jnp.concatenate([seg_ids[0], -1 - jnp.arange(decodes, dtype=jnp.int32)])

    block = min(Q_BLOCK, group_len)
    tops, totals, outs = [], [], []
    for first in range(0, group_len, block):
        low = max(0, ((first - (SEG_MAX - 1)) // K_ALIGN) * K_ALIGN)
        high = first + block
        span = high - low
        query_block = queries[first:high].reshape(block, heads_local, HDIM)
        key_block = keys[low:high].reshape(span, heads_local, HDIM)
        value_block = values[low:high].reshape(span, heads_local, HDIM)
        scores = (
            jnp.einsum("qhe,khe->hqk", query_block, key_block, preferred_element_type=jnp.float32)
            * scale
        )
        query_pos = jnp.arange(first, high, dtype=jnp.int32)
        key_pos = jnp.arange(low, high, dtype=jnp.int32)
        visible = (labels[first:high][:, None] == labels[low:high][None, :]) & (
            key_pos[None, :] <= query_pos[:, None]
        )
        part = softmax_part(scores, visible[None, :, :], value_block, "hqk,khe->qhe")
        tops.append(part[0].T)
        totals.append(part[1].T)
        outs.append(part[2])
    top = jnp.concatenate(tops, axis=0)
    total = jnp.concatenate(totals, axis=0)
    output = jnp.concatenate(outs, axis=0)

    dec_queries = queries[prefill:]
    rows_h = decodes * heads_local
    row_req = jnp.arange(rows_h, dtype=jnp.int32) // heads_local

    pages, page_len = key_pool.shape[0], key_pool.shape[1]
    table = page_table[0]
    own_pages = table.shape[0] // decodes
    slot = page_slots(table, jnp.arange(pages, dtype=jnp.int32))
    owner = jnp.repeat(slot // own_pages, page_len)
    offset = ((slot % own_pages)[:, None] * page_len + jnp.arange(page_len)[None, :]).reshape(-1)
    own_visible = (owner[:, None] == row_req[None, :]) & (
        offset[:, None] < own_len[0][row_req][None, :]
    )
    o_top, o_total, o_out = flat_part(
        block_rows(dec_queries, heads_local),
        key_pool.reshape(pages * page_len, width),
        value_pool.reshape(pages * page_len, width),
        own_visible,
        scale,
    )
    own_part = (
        o_top.reshape(decodes, heads_local),
        o_total.reshape(decodes, heads_local),
        take_heads(o_out, decodes, heads_local),
    )

    data_size = lax.axis_size("dp")
    shifted = [dec_queries] + [
        lax.ppermute(dec_queries, "dp", [(i, (i + k) % data_size) for i in range(data_size)])
        for k in range(1, data_size)
    ]
    source_order = (data_rank - jnp.arange(data_size, dtype=jnp.int32)) % data_size
    all_queries = jnp.take(jnp.stack(shifted), source_order, axis=0).reshape(
        data_size * decodes, width
    )
    all_count = all_queries.shape[0]
    all_rows = all_count * heads_local
    pre_local = prefix_keys.shape[0]
    per_prefix = prefix_table.shape[0] // prefix_len.shape[0]
    page_ids = data_rank * pre_local + jnp.arange(pre_local, dtype=jnp.int32)
    pslot = page_slots(prefix_table, page_ids)
    p_owner = jnp.repeat(pslot // per_prefix, page_len)
    p_offset = (
        (pslot % per_prefix)[:, None] * page_len + jnp.arange(page_len)[None, :]
    ).reshape(-1)
    row_prefix = group_of.reshape(-1)[jnp.arange(all_rows, dtype=jnp.int32) // heads_local]
    p_visible = (p_owner[:, None] == row_prefix[None, :]) & (
        p_offset[:, None] < prefix_len[row_prefix][None, :]
    )
    p_top, p_total, p_out = flat_part(
        block_rows(all_queries, heads_local),
        prefix_keys.reshape(pre_local * page_len, width),
        prefix_values.reshape(pre_local * page_len, width),
        p_visible,
        scale,
    )
    packed = jnp.concatenate(
        [
            take_heads(p_out, all_count, heads_local),
            p_top.reshape(all_count, heads_local, 1),
            p_total.reshape(all_count, heads_local, 1),
        ],
        axis=-1,
    )
    received = [lax.dynamic_slice_in_dim(packed, data_rank * decodes, decodes, axis=0)]
    for k in range(1, data_size):
        target = (data_rank + k) % data_size
        outgoing = lax.dynamic_slice_in_dim(packed, target * decodes, decodes, axis=0)
        received.append(
            lax.ppermute(outgoing, "dp", [(i, (i + k) % data_size) for i in range(data_size)])
        )
    mine = jnp.stack(received)
    m_all = mine[..., HDIM]
    p_max = jnp.max(m_all, axis=0)
    p_scale = jnp.exp(m_all - p_max[None])
    prefix_result = (
        p_max,
        jnp.sum(mine[..., HDIM + 1] * p_scale, axis=0),
        jnp.sum(mine[..., :HDIM] * p_scale[..., None], axis=0),
    )

    batch_dec = (top[prefill:], total[prefill:], output[prefill:])
    merged_dec = combine_parts(combine_parts(batch_dec, own_part), prefix_result)
    total = jnp.concatenate([total[:prefill], merged_dec[1]], axis=0)
    output = jnp.concatenate([output[:prefill], merged_dec[2]], axis=0)
    attention = (output / total[..., None]).reshape(group_len, width).astype(jnp.bfloat16)
    projected = jnp.dot(attention, w_out, preferred_element_type=jnp.float32).astype(jnp.bfloat16)
    state = (tokens.astype(jnp.float32) + scatter_sum(projected)).astype(jnp.bfloat16)
    hidden = jax.nn.gelu(
        jnp.dot(gather_rows(layer_norm(state)), w_up, preferred_element_type=jnp.float32),
        approximate=False,
    ).astype(jnp.bfloat16)
    mlp_part = jnp.dot(hidden, w_down, preferred_element_type=jnp.float32).astype(jnp.bfloat16)
    mlp_share = scatter_sum(mlp_part)
    return (state.astype(jnp.float32) + mlp_share).astype(jnp.bfloat16)


def solution(mesh):
    data_size = mesh.shape["dp"]
    tensor_size = mesh.shape["tensor"]
    split = Mesh(mesh.devices.reshape(data_size, tensor_size // 2, 2), ("dp", "tx", "tc"))
    placed = (
        P(("dp", "tx", "tc"), None),
        P(None, None, ("tx", "tc")),
        P(("tx", "tc"), None),
        P(None, ("tx", "tc")),
        P(("tx", "tc"), None),
        P("dp", None, ("tx", "tc")),
        P("dp", None, ("tx", "tc")),
        P("dp", None, ("tx", "tc")),
        P("dp", None, ("tx", "tc")),
        P("dp", None),
        P("dp", None),
        P(),
        P(),
        P(),
        P("dp", None),
    )
    return jax.shard_map(
        per_device, mesh=split, in_specs=placed, out_specs=P(("dp", "tx", "tc"), None), check_vma=False
    )
```

```python
import jax
import jax.numpy as jnp
from jax import lax
from jax.sharding import Mesh, PartitionSpec as P

HDIM = 64
SEG_MAX = 1020
Q_BLOCK = 512
K_ALIGN = 128


negative_fill = -1e30
epsilon = 1e-05


def layer_norm(matrix):
    values = matrix.astype(jnp.float32)
    average = jnp.mean(values, axis=-1, keepdims=True)
    centred = values - average
    variance = jnp.mean(centred * centred, axis=-1, keepdims=True)
    return (centred * lax.rsqrt(variance + epsilon)).astype(jnp.bfloat16)


def softmax_part(scores, visible, values, pattern):
    top = jnp.max(jnp.where(visible, scores, negative_fill), axis=-1)
    weights = jnp.where(visible, jnp.exp(scores - top[..., None]), 0.0)
    total = jnp.sum(weights, axis=-1)
    output = jnp.einsum(
        pattern, weights.astype(jnp.bfloat16), values, preferred_element_type=jnp.float32
    )
    return (top, total, output)


def combine_parts(first, second):
    top = jnp.maximum(first[0], second[0])
    scale_one = jnp.exp(first[0] - top)
    scale_two = jnp.exp(second[0] - top)
    return (
        top,
        first[1] * scale_one + second[1] * scale_two,
        first[2] * scale_one[..., None] + second[2] * scale_two[..., None],
    )


def block_rows(queries, heads):
    count, width = queries.shape
    rep = jnp.repeat(queries, heads, axis=0)
    row_head = jnp.arange(count * heads, dtype=jnp.int32) % heads
    col_head = jnp.arange(width, dtype=jnp.int32) // HDIM
    return jnp.where(row_head[:, None] == col_head[None, :], rep, jnp.zeros_like(rep))


def take_heads(output, count, heads):
    split = output.reshape(count, heads, heads, HDIM)
    eye = jnp.arange(heads)[:, None] == jnp.arange(heads)[None, :]
    return jnp.sum(jnp.where(eye[None, :, :, None], split, 0.0), axis=2)


def flat_part(query_rows, keys, values, visible, scale):
    scores = (
        lax.dot_general(
            keys, query_rows, (((1,), (1,)), ((), ())), preferred_element_type=jnp.float32
        )
        * scale
    )
    top = jnp.max(jnp.where(visible, scores, negative_fill), axis=0)
    weights = jnp.where(visible, jnp.exp(scores - top[None, :]), 0.0)
    total = jnp.sum(weights, axis=0)
    output = jnp.dot(weights.T.astype(jnp.bfloat16), values, preferred_element_type=jnp.float32)
    return top, total, output


def page_slots(table, page_ids):
    matches = table[:, None] == page_ids[None, :]
    index = jnp.arange(table.shape[0], dtype=jnp.int32)
    return jnp.sum(jnp.where(matches, index[:, None], 0), axis=0)


def ring(axis, shift):
    size = lax.axis_size(axis)
    return [(i, (i + shift) % size) for i in range(size)]


def gather_any(rows):
    chips = lax.axis_size("tx")
    held = jnp.stack(
        [rows] + [lax.ppermute(rows, "tx", ring("tx", k)) for k in range(1, chips)]
    )
    return jnp.stack([held, lax.ppermute(held, "tc", ring("tc", 1))])


def block_order():
    chips = lax.axis_size("tx")
    chip = lax.axis_index("tx")
    core = lax.axis_index("tc")
    step = jnp.arange(chips, dtype=jnp.int32)
    side = jnp.arange(2, dtype=jnp.int32)
    return (((chip - step) % chips)[None, :] * 2 + (core ^ side)[:, None]).reshape(-1)


def gather_rows(rows):
    held = gather_any(rows).reshape(-1, rows.shape[0], rows.shape[1])
    inverse = jnp.argsort(block_order())
    return jnp.take(held, inverse, axis=0).reshape(-1, rows.shape[1])


def scatter_any(partial):
    chips = lax.axis_size("tx")
    chip_sum = partial[0].astype(jnp.float32) + lax.ppermute(
        partial[1], "tc", ring("tc", 1)
    ).astype(jnp.float32)
    chip_half = chip_sum.astype(jnp.bfloat16)
    total = chip_sum[0]
    for k in range(1, chips):
        total = total + lax.ppermute(chip_half[k], "tx", ring("tx", chips - k)).astype(
            jnp.float32
        )
    return total


def per_device(
    tokens,
    w_qkv,
    w_out,
    w_up,
    w_down,
    key_pool,
    value_pool,
    prefix_keys,
    prefix_values,
    page_table,
    own_len,
    group_of,
    prefix_table,
    prefix_len,
    seg_ids,
):
    chips = lax.axis_size("tx")
    cores = lax.axis_size("tc")
    tensor_size = chips * cores
    data_rank = lax.axis_index("dp")
    local_rows = tokens.shape[0]
    group_len = local_rows * tensor_size
    decodes = own_len.shape[1]
    prefill = group_len - decodes
    width = w_out.shape[0]
    heads_local = width // HDIM
    scale = HDIM ** (-0.5)
    normed = gather_rows(layer_norm(tokens))
    qkv = jnp.einsum(
        "td,jde->jte", normed, w_qkv, preferred_element_type=jnp.float32
    ).astype(jnp.bfloat16)
    queries = qkv[0]
    keys = qkv[1]
    values = qkv[2]
    labels = jnp.concatenate([seg_ids[0], -1 - jnp.arange(decodes, dtype=jnp.int32)])

    block = min(Q_BLOCK, group_len)
    tops, totals, outs = [], [], []
    for first in range(0, group_len, block):
        low = max(0, ((first - (SEG_MAX - 1)) // K_ALIGN) * K_ALIGN)
        high = first + block
        span = high - low
        query_block = queries[first:high].reshape(block, heads_local, HDIM)
        key_block = keys[low:high].reshape(span, heads_local, HDIM)
        value_block = values[low:high].reshape(span, heads_local, HDIM)
        scores = (
            jnp.einsum("qhe,khe->hqk", query_block, key_block, preferred_element_type=jnp.float32)
            * scale
        )
        query_pos = jnp.arange(first, high, dtype=jnp.int32)
        key_pos = jnp.arange(low, high, dtype=jnp.int32)
        visible = (labels[first:high][:, None] == labels[low:high][None, :]) & (
            key_pos[None, :] <= query_pos[:, None]
        )
        part = softmax_part(scores, visible[None, :, :], value_block, "hqk,khe->qhe")
        tops.append(part[0].T)
        totals.append(part[1].T)
        outs.append(part[2])
    top = jnp.concatenate(tops, axis=0)
    total = jnp.concatenate(totals, axis=0)
    output = jnp.concatenate(outs, axis=0)

    dec_queries = queries[prefill:]
    rows_h = decodes * heads_local
    row_req = jnp.arange(rows_h, dtype=jnp.int32) // heads_local

    pages, page_len = key_pool.shape[0], key_pool.shape[1]
    table = page_table[0]
    own_pages = table.shape[0] // decodes
    slot = page_slots(table, jnp.arange(pages, dtype=jnp.int32))
    owner = jnp.repeat(slot // own_pages, page_len)
    offset = ((slot % own_pages)[:, None] * page_len + jnp.arange(page_len)[None, :]).reshape(-1)
    own_visible = (owner[:, None] == row_req[None, :]) & (
        offset[:, None] < own_len[0][row_req][None, :]
    )
    o_top, o_total, o_out = flat_part(
        block_rows(dec_queries, heads_local),
        key_pool.reshape(pages * page_len, width),
        value_pool.reshape(pages * page_len, width),
        own_visible,
        scale,
    )
    own_part = (
        o_top.reshape(decodes, heads_local),
        o_total.reshape(decodes, heads_local),
        take_heads(o_out, decodes, heads_local),
    )

    data_size = lax.axis_size("dp")
    shifted = [dec_queries] + [
        lax.ppermute(dec_queries, "dp", [(i, (i + k) % data_size) for i in range(data_size)])
        for k in range(1, data_size)
    ]
    source_order = (data_rank - jnp.arange(data_size, dtype=jnp.int32)) % data_size
    all_queries = jnp.take(jnp.stack(shifted), source_order, axis=0).reshape(
        data_size * decodes, width
    )
    all_count = all_queries.shape[0]
    all_rows = all_count * heads_local
    pre_local = prefix_keys.shape[0]
    per_prefix = prefix_table.shape[0] // prefix_len.shape[0]
    page_ids = data_rank * pre_local + jnp.arange(pre_local, dtype=jnp.int32)
    pslot = page_slots(prefix_table, page_ids)
    p_owner = jnp.repeat(pslot // per_prefix, page_len)
    p_offset = (
        (pslot % per_prefix)[:, None] * page_len + jnp.arange(page_len)[None, :]
    ).reshape(-1)
    row_prefix = group_of.reshape(-1)[jnp.arange(all_rows, dtype=jnp.int32) // heads_local]
    p_visible = (p_owner[:, None] == row_prefix[None, :]) & (
        p_offset[:, None] < prefix_len[row_prefix][None, :]
    )
    p_top, p_total, p_out = flat_part(
        block_rows(all_queries, heads_local),
        prefix_keys.reshape(pre_local * page_len, width),
        prefix_values.reshape(pre_local * page_len, width),
        p_visible,
        scale,
    )
    packed = jnp.concatenate(
        [
            take_heads(p_out, all_count, heads_local),
            p_top.reshape(all_count, heads_local, 1),
            p_total.reshape(all_count, heads_local, 1),
        ],
        axis=-1,
    )
    received = [lax.dynamic_slice_in_dim(packed, data_rank * decodes, decodes, axis=0)]
    for k in range(1, data_size):
        target = (data_rank + k) % data_size
        outgoing = lax.dynamic_slice_in_dim(packed, target * decodes, decodes, axis=0)
        received.append(
            lax.ppermute(outgoing, "dp", [(i, (i + k) % data_size) for i in range(data_size)])
        )
    mine = jnp.stack(received)
    m_all = mine[..., HDIM]
    p_max = jnp.max(m_all, axis=0)
    p_scale = jnp.exp(m_all - p_max[None])
    prefix_result = (
        p_max,
        jnp.sum(mine[..., HDIM + 1] * p_scale, axis=0),
        jnp.sum(mine[..., :HDIM] * p_scale[..., None], axis=0),
    )

    batch_dec = (top[prefill:], total[prefill:], output[prefill:])
    merged_dec = combine_parts(combine_parts(batch_dec, own_part), prefix_result)
    total = jnp.concatenate([total[:prefill], merged_dec[1]], axis=0)
    output = jnp.concatenate([output[:prefill], merged_dec[2]], axis=0)
    attention = (output / total[..., None]).reshape(group_len, width).astype(jnp.bfloat16)
    ordered = jnp.take(attention.reshape(tensor_size, local_rows, width), block_order(), axis=0)
    projected = jnp.dot(
        ordered.reshape(group_len, width), w_out, preferred_element_type=jnp.float32
    ).astype(jnp.bfloat16)
    state = (
        tokens.astype(jnp.float32)
        + scatter_any(projected.reshape(2, chips, local_rows, -1))
    ).astype(jnp.bfloat16)
    state_rows = gather_any(layer_norm(state)).reshape(group_len, -1)
    hidden = jax.nn.gelu(
        jnp.dot(state_rows, w_up, preferred_element_type=jnp.float32), approximate=False
    ).astype(jnp.bfloat16)
    mlp_part = jnp.dot(hidden, w_down, preferred_element_type=jnp.float32).astype(jnp.bfloat16)
    mlp_share = scatter_any(mlp_part.reshape(2, chips, local_rows, -1))
    return (state.astype(jnp.float32) + mlp_share).astype(jnp.bfloat16)


def solution(mesh):
    data_size = mesh.shape["dp"]
    tensor_size = mesh.shape["tensor"]
    split = Mesh(mesh.devices.reshape(data_size, tensor_size // 2, 2), ("dp", "tx", "tc"))
    placed = (
        P(("dp", "tx", "tc"), None),
        P(None, None, ("tx", "tc")),
        P(("tx", "tc"), None),
        P(None, ("tx", "tc")),
        P(("tx", "tc"), None),
        P("dp", None, ("tx", "tc")),
        P("dp", None, ("tx", "tc")),
        P("dp", None, ("tx", "tc")),
        P("dp", None, ("tx", "tc")),
        P("dp", None),
        P("dp", None),
        P(),
        P(),
        P(),
        P("dp", None),
    )
    return jax.shard_map(
        per_device, mesh=split, in_specs=placed, out_specs=P(("dp", "tx", "tc"), None), check_vma=False
    )
```

```python
import jax
import jax.numpy as jnp
from jax import lax
from jax.sharding import Mesh, PartitionSpec as P

HDIM = 64
SEG_MAX = 1020
Q_BLOCK = 512
K_ALIGN = 128


negative_fill = -1e30
epsilon = 1e-05


def layer_norm(matrix):
    values = matrix.astype(jnp.float32)
    average = jnp.mean(values, axis=-1, keepdims=True)
    centred = values - average
    variance = jnp.mean(centred * centred, axis=-1, keepdims=True)
    return (centred * lax.rsqrt(variance + epsilon)).astype(jnp.bfloat16)


def softmax_part(scores, visible, values, pattern):
    top = jnp.max(jnp.where(visible, scores, negative_fill), axis=-1)
    weights = jnp.where(visible, jnp.exp(scores - top[..., None]), 0.0)
    total = jnp.sum(weights, axis=-1)
    output = jnp.einsum(
        pattern, weights.astype(jnp.bfloat16), values, preferred_element_type=jnp.float32
    )
    return (top, total, output)


def combine_parts(first, second):
    top = jnp.maximum(first[0], second[0])
    scale_one = jnp.exp(first[0] - top)
    scale_two = jnp.exp(second[0] - top)
    return (
        top,
        first[1] * scale_one + second[1] * scale_two,
        first[2] * scale_one[..., None] + second[2] * scale_two[..., None],
    )


def block_rows(queries, heads):
    count, width = queries.shape
    rep = jnp.repeat(queries, heads, axis=0)
    row_head = jnp.arange(count * heads, dtype=jnp.int32) % heads
    col_head = jnp.arange(width, dtype=jnp.int32) // HDIM
    return jnp.where(row_head[:, None] == col_head[None, :], rep, jnp.zeros_like(rep))


def take_heads(output, count, heads):
    split = output.reshape(count, heads, heads, HDIM)
    eye = jnp.arange(heads)[:, None] == jnp.arange(heads)[None, :]
    return jnp.sum(jnp.where(eye[None, :, :, None], split, 0.0), axis=2)


def flat_part(query_rows, keys, values, visible, scale):
    scores = (
        lax.dot_general(
            keys, query_rows, (((1,), (1,)), ((), ())), preferred_element_type=jnp.float32
        )
        * scale
    )
    top = jnp.max(jnp.where(visible, scores, negative_fill), axis=0)
    weights = jnp.where(visible, jnp.exp(scores - top[None, :]), 0.0)
    total = jnp.sum(weights, axis=0)
    output = jnp.dot(weights.T.astype(jnp.bfloat16), values, preferred_element_type=jnp.float32)
    return top, total, output


def page_slots(table, page_ids):
    matches = table[:, None] == page_ids[None, :]
    index = jnp.arange(table.shape[0], dtype=jnp.int32)
    return jnp.sum(jnp.where(matches, index[:, None], 0), axis=0)


def ring(axis, shift):
    size = lax.axis_size(axis)
    return [(i, (i + shift) % size) for i in range(size)]


def gather_any(rows):
    chips = lax.axis_size("tx")
    held = jnp.stack(
        [rows] + [lax.ppermute(rows, "tx", ring("tx", k)) for k in range(1, chips)]
    )
    return jnp.stack([held, lax.ppermute(held, "tc", ring("tc", 1))])


def block_order():
    chips = lax.axis_size("tx")
    chip = lax.axis_index("tx")
    core = lax.axis_index("tc")
    step = jnp.arange(chips, dtype=jnp.int32)
    side = jnp.arange(2, dtype=jnp.int32)
    return (((chip - step) % chips)[None, :] * 2 + (core ^ side)[:, None]).reshape(-1)


def gather_rows(rows):
    held = gather_any(rows).reshape(-1, rows.shape[0], rows.shape[1])
    inverse = jnp.argsort(block_order())
    return jnp.take(held, inverse, axis=0).reshape(-1, rows.shape[1])


def scatter_any(partial):
    chips = lax.axis_size("tx")
    chip_sum = partial[0].astype(jnp.float32) + lax.ppermute(
        partial[1], "tc", ring("tc", 1)
    ).astype(jnp.float32)
    chip_half = chip_sum.astype(jnp.bfloat16)
    total = chip_sum[0]
    for k in range(1, chips):
        total = total + lax.ppermute(chip_half[k], "tx", ring("tx", chips - k)).astype(
            jnp.float32
        )
    return total


def per_device(
    tokens,
    w_qkv,
    w_out,
    w_up,
    w_down,
    key_pool,
    value_pool,
    prefix_keys,
    prefix_values,
    page_table,
    own_len,
    group_of,
    prefix_table,
    prefix_len,
    seg_ids,
):
    chips = lax.axis_size("tx")
    cores = lax.axis_size("tc")
    tensor_size = chips * cores
    data_rank = lax.axis_index("dp")
    local_rows = tokens.shape[0]
    group_len = local_rows * tensor_size
    decodes = own_len.shape[1]
    prefill = group_len - decodes
    width = w_out.shape[0]
    heads_local = width // HDIM
    scale = HDIM ** (-0.5)
    normed = gather_rows(layer_norm(tokens))
    qkv = jnp.einsum(
        "td,jde->jte", normed, w_qkv, preferred_element_type=jnp.float32
    ).astype(jnp.bfloat16)
    queries = qkv[0]
    keys = qkv[1]
    values = qkv[2]
    labels = jnp.concatenate([seg_ids[0], -1 - jnp.arange(decodes, dtype=jnp.int32)])

    block = min(Q_BLOCK, group_len)
    tops, totals, outs = [], [], []
    for first in range(0, group_len, block):
        low = max(0, ((first - (SEG_MAX - 1)) // K_ALIGN) * K_ALIGN)
        high = first + block
        span = high - low
        query_block = queries[first:high].reshape(block, heads_local, HDIM)
        key_block = keys[low:high].reshape(span, heads_local, HDIM)
        value_block = values[low:high].reshape(span, heads_local, HDIM)
        scores = (
            jnp.einsum("qhe,khe->hqk", query_block, key_block, preferred_element_type=jnp.float32)
            * scale
        )
        query_pos = jnp.arange(first, high, dtype=jnp.int32)
        key_pos = jnp.arange(low, high, dtype=jnp.int32)
        visible = (labels[first:high][:, None] == labels[low:high][None, :]) & (
            key_pos[None, :] <= query_pos[:, None]
        )
        part = softmax_part(scores, visible[None, :, :], value_block, "hqk,khe->qhe")
        tops.append(part[0].T)
        totals.append(part[1].T)
        outs.append(part[2])
    top = jnp.concatenate(tops, axis=0)
    total = jnp.concatenate(totals, axis=0)
    output = jnp.concatenate(outs, axis=0)

    dec_queries = queries[prefill:]
    rows_h = decodes * heads_local
    row_req = jnp.arange(rows_h, dtype=jnp.int32) // heads_local

    pages, page_len = key_pool.shape[0], key_pool.shape[1]
    table = page_table[0]
    own_pages = table.shape[0] // decodes
    slot = page_slots(table, jnp.arange(pages, dtype=jnp.int32))
    owner = jnp.repeat(slot // own_pages, page_len)
    offset = ((slot % own_pages)[:, None] * page_len + jnp.arange(page_len)[None, :]).reshape(-1)
    own_visible = (owner[:, None] == row_req[None, :]) & (
        offset[:, None] < own_len[0][row_req][None, :]
    )
    o_top, o_total, o_out = flat_part(
        block_rows(dec_queries, heads_local),
        key_pool.reshape(pages * page_len, width),
        value_pool.reshape(pages * page_len, width),
        own_visible,
        scale,
    )
    own_part = (
        o_top.reshape(decodes, heads_local),
        o_total.reshape(decodes, heads_local),
        take_heads(o_out, decodes, heads_local),
    )

    data_size = lax.axis_size("dp")
    shifted = [dec_queries] + [
        lax.ppermute(dec_queries, "dp", [(i, (i + k) % data_size) for i in range(data_size)])
        for k in range(1, data_size)
    ]
    source_order = (data_rank - jnp.arange(data_size, dtype=jnp.int32)) % data_size
    all_queries = jnp.take(jnp.stack(shifted), source_order, axis=0).reshape(
        data_size * decodes, width
    )
    all_count = all_queries.shape[0]
    all_rows = all_count * heads_local
    pre_local = prefix_keys.shape[0]
    per_prefix = prefix_table.shape[0] // prefix_len.shape[0]
    page_ids = data_rank * pre_local + jnp.arange(pre_local, dtype=jnp.int32)
    pslot = page_slots(prefix_table, page_ids)
    p_owner = jnp.repeat(pslot // per_prefix, page_len)
    p_offset = (
        (pslot % per_prefix)[:, None] * page_len + jnp.arange(page_len)[None, :]
    ).reshape(-1)
    row_prefix = group_of.reshape(-1)[jnp.arange(all_rows, dtype=jnp.int32) // heads_local]
    p_visible = (p_owner[:, None] == row_prefix[None, :]) & (
        p_offset[:, None] < prefix_len[row_prefix][None, :]
    )
    p_top, p_total, p_out = flat_part(
        block_rows(all_queries, heads_local),
        prefix_keys.reshape(pre_local * page_len, width),
        prefix_values.reshape(pre_local * page_len, width),
        p_visible,
        scale,
    )
    packed = jnp.concatenate(
        [
            take_heads(p_out, all_count, heads_local),
            p_top.reshape(all_count, heads_local, 1),
            p_total.reshape(all_count, heads_local, 1),
        ],
        axis=-1,
    )
    received = [lax.dynamic_slice_in_dim(packed, data_rank * decodes, decodes, axis=0)]
    for k in range(1, data_size):
        target = (data_rank + k) % data_size
        outgoing = lax.dynamic_slice_in_dim(packed, target * decodes, decodes, axis=0)
        received.append(
            lax.ppermute(outgoing, "dp", [(i, (i + k) % data_size) for i in range(data_size)])
        )
    mine = jnp.stack(received)
    m_all = mine[..., HDIM]
    p_max = jnp.max(m_all, axis=0)
    p_scale = jnp.exp(m_all - p_max[None])
    prefix_result = (
        p_max,
        jnp.sum(mine[..., HDIM + 1] * p_scale, axis=0),
        jnp.sum(mine[..., :HDIM] * p_scale[..., None], axis=0),
    )

    batch_dec = (top[prefill:], total[prefill:], output[prefill:])
    merged_dec = combine_parts(combine_parts(batch_dec, own_part), prefix_result)
    total = jnp.concatenate([total[:prefill], merged_dec[1]], axis=0)
    output = jnp.concatenate([output[:prefill], merged_dec[2]], axis=0)
    attention = (output / total[..., None]).reshape(group_len, width).astype(jnp.bfloat16)
    order = block_order()
    projected = jnp.stack(
        [
            jnp.dot(
                lax.dynamic_slice_in_dim(attention, order[j] * local_rows, local_rows, 0),
                w_out,
                preferred_element_type=jnp.float32,
            ).astype(jnp.bfloat16)
            for j in range(tensor_size)
        ]
    )
    state = (
        tokens.astype(jnp.float32)
        + scatter_any(projected.reshape(2, chips, local_rows, -1))
    ).astype(jnp.bfloat16)
    state_rows = gather_any(layer_norm(state)).reshape(group_len, -1)
    hidden = jax.nn.gelu(
        jnp.dot(state_rows, w_up, preferred_element_type=jnp.float32), approximate=False
    ).astype(jnp.bfloat16)
    mlp_part = jnp.dot(hidden, w_down, preferred_element_type=jnp.float32).astype(jnp.bfloat16)
    mlp_share = scatter_any(mlp_part.reshape(2, chips, local_rows, -1))
    return (state.astype(jnp.float32) + mlp_share).astype(jnp.bfloat16)


def solution(mesh):
    data_size = mesh.shape["dp"]
    tensor_size = mesh.shape["tensor"]
    split = Mesh(mesh.devices.reshape(data_size, tensor_size // 2, 2), ("dp", "tx", "tc"))
    placed = (
        P(("dp", "tx", "tc"), None),
        P(None, None, ("tx", "tc")),
        P(("tx", "tc"), None),
        P(None, ("tx", "tc")),
        P(("tx", "tc"), None),
        P("dp", None, ("tx", "tc")),
        P("dp", None, ("tx", "tc")),
        P("dp", None, ("tx", "tc")),
        P("dp", None, ("tx", "tc")),
        P("dp", None),
        P("dp", None),
        P(),
        P(),
        P(),
        P("dp", None),
    )
    return jax.shard_map(
        per_device, mesh=split, in_specs=placed, out_specs=P(("dp", "tx", "tc"), None), check_vma=False
    )
```

```python
import jax
import jax.numpy as jnp
from jax import lax
from jax.sharding import Mesh, PartitionSpec as P

HDIM = 64
SEG_MAX = 1020


negative_fill = -1e30
epsilon = 1e-05


def layer_norm(matrix):
    values = matrix.astype(jnp.float32)
    average = jnp.mean(values, axis=-1, keepdims=True)
    centred = values - average
    variance = jnp.mean(centred * centred, axis=-1, keepdims=True)
    return (centred * lax.rsqrt(variance + epsilon)).astype(jnp.bfloat16)


def softmax_part(scores, visible, values, pattern):
    top = jnp.max(jnp.where(visible, scores, negative_fill), axis=-1)
    weights = jnp.where(visible, jnp.exp(scores - top[..., None]), 0.0)
    total = jnp.sum(weights, axis=-1)
    output = jnp.einsum(
        pattern, weights.astype(jnp.bfloat16), values, preferred_element_type=jnp.float32
    )
    return (top, total, output)


def combine_parts(first, second):
    top = jnp.maximum(first[0], second[0])
    scale_one = jnp.exp(first[0] - top)
    scale_two = jnp.exp(second[0] - top)
    return (
        top,
        first[1] * scale_one + second[1] * scale_two,
        first[2] * scale_one[..., None] + second[2] * scale_two[..., None],
    )


def block_rows(queries, heads):
    count, width = queries.shape
    rep = jnp.repeat(queries, heads, axis=0)
    row_head = jnp.arange(count * heads, dtype=jnp.int32) % heads
    col_head = jnp.arange(width, dtype=jnp.int32) // HDIM
    return jnp.where(row_head[:, None] == col_head[None, :], rep, jnp.zeros_like(rep))


def take_heads(output, count, heads):
    split = output.reshape(count, heads, heads, HDIM)
    eye = jnp.arange(heads)[:, None] == jnp.arange(heads)[None, :]
    return jnp.sum(jnp.where(eye[None, :, :, None], split, 0.0), axis=2)


def flat_part(query_rows, keys, values, visible, scale):
    scores = (
        lax.dot_general(
            keys, query_rows, (((1,), (1,)), ((), ())), preferred_element_type=jnp.float32
        )
        * scale
    )
    top = jnp.max(jnp.where(visible, scores, negative_fill), axis=0)
    weights = jnp.where(visible, jnp.exp(scores - top[None, :]), 0.0)
    total = jnp.sum(weights, axis=0)
    output = jnp.dot(weights.T.astype(jnp.bfloat16), values, preferred_element_type=jnp.float32)
    return top, total, output


def page_slots(table, page_ids):
    matches = table[:, None] == page_ids[None, :]
    index = jnp.arange(table.shape[0], dtype=jnp.int32)
    return jnp.sum(jnp.where(matches, index[:, None], 0), axis=0)


def ring(axis, shift):
    size = lax.axis_size(axis)
    return [(i, (i + shift) % size) for i in range(size)]


def gather_any(rows):
    chips = lax.axis_size("tx")
    held = jnp.stack(
        [rows] + [lax.ppermute(rows, "tx", ring("tx", k)) for k in range(1, chips)]
    )
    return jnp.stack([held, lax.ppermute(held, "tc", ring("tc", 1))])


def block_order():
    chips = lax.axis_size("tx")
    chip = lax.axis_index("tx")
    core = lax.axis_index("tc")
    step = jnp.arange(chips, dtype=jnp.int32)
    side = jnp.arange(2, dtype=jnp.int32)
    return (((chip - step) % chips)[None, :] * 2 + (core ^ side)[:, None]).reshape(-1)


def scatter_any(partial):
    chips = lax.axis_size("tx")
    chip_sum = partial[0].astype(jnp.float32) + lax.ppermute(
        partial[1], "tc", ring("tc", 1)
    ).astype(jnp.float32)
    chip_half = chip_sum.astype(jnp.bfloat16)
    total = chip_sum[0]
    for k in range(1, chips):
        total = total + lax.ppermute(chip_half[k], "tx", ring("tx", chips - k)).astype(
            jnp.float32
        )
    return total


def per_device(
    tokens,
    w_qkv,
    w_out,
    w_up,
    w_down,
    key_pool,
    value_pool,
    prefix_keys,
    prefix_values,
    page_table,
    own_len,
    group_of,
    prefix_table,
    prefix_len,
    seg_ids,
):
    chips = lax.axis_size("tx")
    cores = lax.axis_size("tc")
    tensor_size = chips * cores
    data_rank = lax.axis_index("dp")
    local_rows = tokens.shape[0]
    group_len = local_rows * tensor_size
    decodes = own_len.shape[1]
    prefill = group_len - decodes
    width = w_out.shape[0]
    heads_local = width // HDIM
    scale = HDIM ** (-0.5)
    pieces = gather_any(layer_norm(tokens)).reshape(tensor_size, local_rows, -1)
    qkv = jnp.einsum(
        "jtd,kde->kjte", pieces, w_qkv, preferred_element_type=jnp.float32
    ).astype(jnp.bfloat16)
    order = block_order()
    inverse = jnp.argsort(order)

    def block_of(kind, index):
        return lax.dynamic_index_in_dim(qkv[kind], inverse[index], 0, keepdims=False)

    labels = jnp.concatenate([seg_ids[0], -1 - jnp.arange(decodes, dtype=jnp.int32)])

    block = local_rows
    tops, totals, outs = [], [], []
    for index in range(tensor_size):
        first = index * block
        low_block = max(0, (first - (SEG_MAX - 1)) // block)
        low = low_block * block
        high = first + block
        span = high - low
        query_block = block_of(0, index).reshape(block, heads_local, HDIM)
        key_block = jnp.concatenate(
            [block_of(1, b) for b in range(low_block, index + 1)], axis=0
        ).reshape(span, heads_local, HDIM)
        value_block = jnp.concatenate(
            [block_of(2, b) for b in range(low_block, index + 1)], axis=0
        ).reshape(span, heads_local, HDIM)
        scores = (
            jnp.einsum("qhe,khe->hqk", query_block, key_block, preferred_element_type=jnp.float32)
            * scale
        )
        query_pos = jnp.arange(first, high, dtype=jnp.int32)
        key_pos = jnp.arange(low, high, dtype=jnp.int32)
        visible = (labels[first:high][:, None] == labels[low:high][None, :]) & (
            key_pos[None, :] <= query_pos[:, None]
        )
        part = softmax_part(scores, visible[None, :, :], value_block, "hqk,khe->qhe")
        tops.append(part[0].T)
        totals.append(part[1].T)
        outs.append(part[2])
    top = jnp.concatenate(tops, axis=0)
    total = jnp.concatenate(totals, axis=0)
    output = jnp.concatenate(outs, axis=0)

    dec_queries = block_of(0, tensor_size - 1)[local_rows - decodes :]
    rows_h = decodes * heads_local
    row_req = jnp.arange(rows_h, dtype=jnp.int32) // heads_local

    pages, page_len = key_pool.shape[0], key_pool.shape[1]
    table = page_table[0]
    own_pages = table.shape[0] // decodes
    slot = page_slots(table, jnp.arange(pages, dtype=jnp.int32))
    owner = jnp.repeat(slot // own_pages, page_len)
    offset = ((slot % own_pages)[:, None] * page_len + jnp.arange(page_len)[None, :]).reshape(-1)
    own_visible = (owner[:, None] == row_req[None, :]) & (
        offset[:, None] < own_len[0][row_req][None, :]
    )
    o_top, o_total, o_out = flat_part(
        block_rows(dec_queries, heads_local),
        key_pool.reshape(pages * page_len, width),
        value_pool.reshape(pages * page_len, width),
        own_visible,
        scale,
    )
    own_part = (
        o_top.reshape(decodes, heads_local),
        o_total.reshape(decodes, heads_local),
        take_heads(o_out, decodes, heads_local),
    )

    data_size = lax.axis_size("dp")
    shifted = [dec_queries] + [
        lax.ppermute(dec_queries, "dp", [(i, (i + k) % data_size) for i in range(data_size)])
        for k in range(1, data_size)
    ]
    source_order = (data_rank - jnp.arange(data_size, dtype=jnp.int32)) % data_size
    all_queries = jnp.take(jnp.stack(shifted), source_order, axis=0).reshape(
        data_size * decodes, width
    )
    all_count = all_queries.shape[0]
    all_rows = all_count * heads_local
    pre_local = prefix_keys.shape[0]
    per_prefix = prefix_table.shape[0] // prefix_len.shape[0]
    page_ids = data_rank * pre_local + jnp.arange(pre_local, dtype=jnp.int32)
    pslot = page_slots(prefix_table, page_ids)
    p_owner = jnp.repeat(pslot // per_prefix, page_len)
    p_offset = (
        (pslot % per_prefix)[:, None] * page_len + jnp.arange(page_len)[None, :]
    ).reshape(-1)
    row_prefix = group_of.reshape(-1)[jnp.arange(all_rows, dtype=jnp.int32) // heads_local]
    p_visible = (p_owner[:, None] == row_prefix[None, :]) & (
        p_offset[:, None] < prefix_len[row_prefix][None, :]
    )
    p_top, p_total, p_out = flat_part(
        block_rows(all_queries, heads_local),
        prefix_keys.reshape(pre_local * page_len, width),
        prefix_values.reshape(pre_local * page_len, width),
        p_visible,
        scale,
    )
    packed = jnp.concatenate(
        [
            take_heads(p_out, all_count, heads_local),
            p_top.reshape(all_count, heads_local, 1),
            p_total.reshape(all_count, heads_local, 1),
        ],
        axis=-1,
    )
    received = [lax.dynamic_slice_in_dim(packed, data_rank * decodes, decodes, axis=0)]
    for k in range(1, data_size):
        target = (data_rank + k) % data_size
        outgoing = lax.dynamic_slice_in_dim(packed, target * decodes, decodes, axis=0)
        received.append(
            lax.ppermute(outgoing, "dp", [(i, (i + k) % data_size) for i in range(data_size)])
        )
    mine = jnp.stack(received)
    m_all = mine[..., HDIM]
    p_max = jnp.max(m_all, axis=0)
    p_scale = jnp.exp(m_all - p_max[None])
    prefix_result = (
        p_max,
        jnp.sum(mine[..., HDIM + 1] * p_scale, axis=0),
        jnp.sum(mine[..., :HDIM] * p_scale[..., None], axis=0),
    )

    batch_dec = (top[prefill:], total[prefill:], output[prefill:])
    merged_dec = combine_parts(combine_parts(batch_dec, own_part), prefix_result)
    total = jnp.concatenate([total[:prefill], merged_dec[1]], axis=0)
    output = jnp.concatenate([output[:prefill], merged_dec[2]], axis=0)
    attention = (output / total[..., None]).reshape(group_len, width).astype(jnp.bfloat16)
    projected = jnp.stack(
        [
            jnp.dot(
                lax.dynamic_slice_in_dim(attention, order[j] * local_rows, local_rows, 0),
                w_out,
                preferred_element_type=jnp.float32,
            ).astype(jnp.bfloat16)
            for j in range(tensor_size)
        ]
    )
    state = (
        tokens.astype(jnp.float32)
        + scatter_any(projected.reshape(2, chips, local_rows, -1))
    ).astype(jnp.bfloat16)
    state_rows = gather_any(layer_norm(state)).reshape(group_len, -1)
    hidden = jax.nn.gelu(
        jnp.dot(state_rows, w_up, preferred_element_type=jnp.float32), approximate=False
    ).astype(jnp.bfloat16)
    mlp_part = jnp.dot(hidden, w_down, preferred_element_type=jnp.float32).astype(jnp.bfloat16)
    mlp_share = scatter_any(mlp_part.reshape(2, chips, local_rows, -1))
    return (state.astype(jnp.float32) + mlp_share).astype(jnp.bfloat16)


def solution(mesh):
    data_size = mesh.shape["dp"]
    tensor_size = mesh.shape["tensor"]
    split = Mesh(mesh.devices.reshape(data_size, tensor_size // 2, 2), ("dp", "tx", "tc"))
    placed = (
        P(("dp", "tx", "tc"), None),
        P(None, None, ("tx", "tc")),
        P(("tx", "tc"), None),
        P(None, ("tx", "tc")),
        P(("tx", "tc"), None),
        P("dp", None, ("tx", "tc")),
        P("dp", None, ("tx", "tc")),
        P("dp", None, ("tx", "tc")),
        P("dp", None, ("tx", "tc")),
        P("dp", None),
        P("dp", None),
        P(),
        P(),
        P(),
        P("dp", None),
    )
    return jax.shard_map(
        per_device, mesh=split, in_specs=placed, out_specs=P(("dp", "tx", "tc"), None), check_vma=False
    )
```

```python
import jax
import jax.numpy as jnp
from jax import lax
from jax.sharding import Mesh, PartitionSpec as P

HDIM = 64
SEG_MAX = 1020


negative_fill = -1e30
epsilon = 1e-05


def layer_norm(matrix):
    values = matrix.astype(jnp.float32)
    average = jnp.mean(values, axis=-1, keepdims=True)
    centred = values - average
    variance = jnp.mean(centred * centred, axis=-1, keepdims=True)
    return (centred * lax.rsqrt(variance + epsilon)).astype(jnp.bfloat16)


def softmax_part(scores, visible, values, pattern):
    top = jnp.max(jnp.where(visible, scores, negative_fill), axis=-1)
    weights = jnp.where(visible, jnp.exp(scores - top[..., None]), 0.0)
    total = jnp.sum(weights, axis=-1)
    output = jnp.einsum(
        pattern, weights.astype(jnp.bfloat16), values, preferred_element_type=jnp.float32
    )
    return (top, total, output)


def combine_parts(first, second):
    top = jnp.maximum(first[0], second[0])
    scale_one = jnp.exp(first[0] - top)
    scale_two = jnp.exp(second[0] - top)
    return (
        top,
        first[1] * scale_one + second[1] * scale_two,
        first[2] * scale_one[..., None] + second[2] * scale_two[..., None],
    )


def block_rows(queries, heads):
    count, width = queries.shape
    rep = jnp.repeat(queries, heads, axis=0)
    row_head = jnp.arange(count * heads, dtype=jnp.int32) % heads
    col_head = jnp.arange(width, dtype=jnp.int32) // HDIM
    return jnp.where(row_head[:, None] == col_head[None, :], rep, jnp.zeros_like(rep))


def take_heads(output, count, heads):
    split = output.reshape(count, heads, heads, HDIM)
    eye = jnp.arange(heads)[:, None] == jnp.arange(heads)[None, :]
    return jnp.sum(jnp.where(eye[None, :, :, None], split, 0.0), axis=2)


def flat_part(query_rows, keys, values, visible, scale):
    scores = (
        lax.dot_general(
            keys, query_rows, (((1,), (1,)), ((), ())), preferred_element_type=jnp.float32
        )
        * scale
    )
    top = jnp.max(jnp.where(visible, scores, negative_fill), axis=0)
    weights = jnp.where(visible, jnp.exp(scores - top[None, :]), 0.0)
    total = jnp.sum(weights, axis=0)
    output = jnp.dot(weights.T.astype(jnp.bfloat16), values, preferred_element_type=jnp.float32)
    return top, total, output


def page_slots(table, page_ids):
    matches = table[:, None] == page_ids[None, :]
    index = jnp.arange(table.shape[0], dtype=jnp.int32)
    return jnp.sum(jnp.where(matches, index[:, None], 0), axis=0)


def ring(axis, shift):
    size = lax.axis_size(axis)
    return [(i, (i + shift) % size) for i in range(size)]


def gather_any(rows):
    chips = lax.axis_size("tx")
    held = jnp.stack(
        [rows] + [lax.ppermute(rows, "tx", ring("tx", k)) for k in range(1, chips)]
    )
    return jnp.stack([held, lax.ppermute(held, "tc", ring("tc", 1))])


def block_order():
    chips = lax.axis_size("tx")
    chip = lax.axis_index("tx")
    core = lax.axis_index("tc")
    step = jnp.arange(chips, dtype=jnp.int32)
    side = jnp.arange(2, dtype=jnp.int32)
    return (((chip - step) % chips)[None, :] * 2 + (core ^ side)[:, None]).reshape(-1)


def scatter_any(partial):
    chips = lax.axis_size("tx")
    chip_sum = partial[0].astype(jnp.float32) + lax.ppermute(
        partial[1], "tc", ring("tc", 1)
    ).astype(jnp.float32)
    chip_half = chip_sum.astype(jnp.bfloat16)
    total = chip_sum[0]
    for k in range(1, chips):
        total = total + lax.ppermute(chip_half[k], "tx", ring("tx", chips - k)).astype(
            jnp.float32
        )
    return total


def per_device(
    tokens,
    w_qkv,
    w_out,
    w_up,
    w_down,
    key_pool,
    value_pool,
    prefix_keys,
    prefix_values,
    page_table,
    own_len,
    group_of,
    prefix_table,
    prefix_len,
    seg_ids,
):
    chips = lax.axis_size("tx")
    cores = lax.axis_size("tc")
    tensor_size = chips * cores
    data_rank = lax.axis_index("dp")
    local_rows = tokens.shape[0]
    group_len = local_rows * tensor_size
    decodes = own_len.shape[1]
    prefill = group_len - decodes
    width = w_out.shape[0]
    heads_local = width // HDIM
    scale = HDIM ** (-0.5)
    pieces = gather_any(layer_norm(tokens)).reshape(tensor_size, local_rows, -1)
    qkv = jnp.einsum(
        "jtd,kde->kjte", pieces, w_qkv, preferred_element_type=jnp.float32
    ).astype(jnp.bfloat16)
    order = block_order()
    inverse = jnp.argsort(order)

    def block_of(kind, index):
        return lax.dynamic_index_in_dim(qkv[kind], inverse[index], 0, keepdims=False)

    dec_queries = lax.dynamic_index_in_dim(
        qkv[0], inverse[tensor_size - 1], 0, keepdims=False
    )[local_rows - decodes :]
    rows_h = decodes * heads_local
    row_req = jnp.arange(rows_h, dtype=jnp.int32) // heads_local

    pages, page_len = key_pool.shape[0], key_pool.shape[1]
    table = page_table[0]
    own_pages = table.shape[0] // decodes
    slot = page_slots(table, jnp.arange(pages, dtype=jnp.int32))
    owner = jnp.repeat(slot // own_pages, page_len)
    offset = ((slot % own_pages)[:, None] * page_len + jnp.arange(page_len)[None, :]).reshape(-1)
    own_visible = (owner[:, None] == row_req[None, :]) & (
        offset[:, None] < own_len[0][row_req][None, :]
    )
    o_top, o_total, o_out = flat_part(
        block_rows(dec_queries, heads_local),
        key_pool.reshape(pages * page_len, width),
        value_pool.reshape(pages * page_len, width),
        own_visible,
        scale,
    )
    own_part = (
        o_top.reshape(decodes, heads_local),
        o_total.reshape(decodes, heads_local),
        take_heads(o_out, decodes, heads_local),
    )

    data_size = lax.axis_size("dp")
    shifted = [dec_queries] + [
        lax.ppermute(dec_queries, "dp", [(i, (i + k) % data_size) for i in range(data_size)])
        for k in range(1, data_size)
    ]
    source_order = (data_rank - jnp.arange(data_size, dtype=jnp.int32)) % data_size
    all_queries = jnp.take(jnp.stack(shifted), source_order, axis=0).reshape(
        data_size * decodes, width
    )
    all_count = all_queries.shape[0]
    all_rows = all_count * heads_local
    pre_local = prefix_keys.shape[0]
    per_prefix = prefix_table.shape[0] // prefix_len.shape[0]
    page_ids = data_rank * pre_local + jnp.arange(pre_local, dtype=jnp.int32)
    pslot = page_slots(prefix_table, page_ids)
    p_owner = jnp.repeat(pslot // per_prefix, page_len)
    p_offset = (
        (pslot % per_prefix)[:, None] * page_len + jnp.arange(page_len)[None, :]
    ).reshape(-1)
    row_prefix = group_of.reshape(-1)[jnp.arange(all_rows, dtype=jnp.int32) // heads_local]
    p_visible = (p_owner[:, None] == row_prefix[None, :]) & (
        p_offset[:, None] < prefix_len[row_prefix][None, :]
    )
    p_top, p_total, p_out = flat_part(
        block_rows(all_queries, heads_local),
        prefix_keys.reshape(pre_local * page_len, width),
        prefix_values.reshape(pre_local * page_len, width),
        p_visible,
        scale,
    )
    packed = jnp.concatenate(
        [
            take_heads(p_out, all_count, heads_local),
            p_top.reshape(all_count, heads_local, 1),
            p_total.reshape(all_count, heads_local, 1),
        ],
        axis=-1,
    )
    packed, qkv = lax.optimization_barrier((packed, qkv))
    labels = jnp.concatenate([seg_ids[0], -1 - jnp.arange(decodes, dtype=jnp.int32)])

    block = local_rows
    tops, totals, outs = [], [], []
    for index in range(tensor_size):
        first = index * block
        low_block = max(0, (first - (SEG_MAX - 1)) // block)
        low = low_block * block
        high = first + block
        span = high - low
        query_block = block_of(0, index).reshape(block, heads_local, HDIM)
        key_block = jnp.concatenate(
            [block_of(1, b) for b in range(low_block, index + 1)], axis=0
        ).reshape(span, heads_local, HDIM)
        value_block = jnp.concatenate(
            [block_of(2, b) for b in range(low_block, index + 1)], axis=0
        ).reshape(span, heads_local, HDIM)
        scores = (
            jnp.einsum("qhe,khe->hqk", query_block, key_block, preferred_element_type=jnp.float32)
            * scale
        )
        query_pos = jnp.arange(first, high, dtype=jnp.int32)
        key_pos = jnp.arange(low, high, dtype=jnp.int32)
        visible = (labels[first:high][:, None] == labels[low:high][None, :]) & (
            key_pos[None, :] <= query_pos[:, None]
        )
        part = softmax_part(scores, visible[None, :, :], value_block, "hqk,khe->qhe")
        tops.append(part[0].T)
        totals.append(part[1].T)
        outs.append(part[2])
    top = jnp.concatenate(tops, axis=0)
    total = jnp.concatenate(totals, axis=0)
    output = jnp.concatenate(outs, axis=0)

    received = [lax.dynamic_slice_in_dim(packed, data_rank * decodes, decodes, axis=0)]
    for k in range(1, data_size):
        target = (data_rank + k) % data_size
        outgoing = lax.dynamic_slice_in_dim(packed, target * decodes, decodes, axis=0)
        received.append(
            lax.ppermute(outgoing, "dp", [(i, (i + k) % data_size) for i in range(data_size)])
        )
    mine = jnp.stack(received)
    m_all = mine[..., HDIM]
    p_max = jnp.max(m_all, axis=0)
    p_scale = jnp.exp(m_all - p_max[None])
    prefix_result = (
        p_max,
        jnp.sum(mine[..., HDIM + 1] * p_scale, axis=0),
        jnp.sum(mine[..., :HDIM] * p_scale[..., None], axis=0),
    )

    batch_dec = (top[prefill:], total[prefill:], output[prefill:])
    merged_dec = combine_parts(combine_parts(batch_dec, own_part), prefix_result)
    total = jnp.concatenate([total[:prefill], merged_dec[1]], axis=0)
    output = jnp.concatenate([output[:prefill], merged_dec[2]], axis=0)
    attention = (output / total[..., None]).reshape(group_len, width).astype(jnp.bfloat16)
    projected = jnp.stack(
        [
            jnp.dot(
                lax.dynamic_slice_in_dim(attention, order[j] * local_rows, local_rows, 0),
                w_out,
                preferred_element_type=jnp.float32,
            ).astype(jnp.bfloat16)
            for j in range(tensor_size)
        ]
    )
    state = (
        tokens.astype(jnp.float32)
        + scatter_any(projected.reshape(2, chips, local_rows, -1))
    ).astype(jnp.bfloat16)
    state_rows = gather_any(layer_norm(state)).reshape(group_len, -1)
    hidden = jax.nn.gelu(
        jnp.dot(state_rows, w_up, preferred_element_type=jnp.float32), approximate=False
    ).astype(jnp.bfloat16)
    mlp_part = jnp.dot(hidden, w_down, preferred_element_type=jnp.float32).astype(jnp.bfloat16)
    mlp_share = scatter_any(mlp_part.reshape(2, chips, local_rows, -1))
    return (state.astype(jnp.float32) + mlp_share).astype(jnp.bfloat16)


def solution(mesh):
    data_size = mesh.shape["dp"]
    tensor_size = mesh.shape["tensor"]
    split = Mesh(mesh.devices.reshape(data_size, tensor_size // 2, 2), ("dp", "tx", "tc"))
    placed = (
        P(("dp", "tx", "tc"), None),
        P(None, None, ("tx", "tc")),
        P(("tx", "tc"), None),
        P(None, ("tx", "tc")),
        P(("tx", "tc"), None),
        P("dp", None, ("tx", "tc")),
        P("dp", None, ("tx", "tc")),
        P("dp", None, ("tx", "tc")),
        P("dp", None, ("tx", "tc")),
        P("dp", None),
        P("dp", None),
        P(),
        P(),
        P(),
        P("dp", None),
    )
    return jax.shard_map(
        per_device, mesh=split, in_specs=placed, out_specs=P(("dp", "tx", "tc"), None), check_vma=False
    )
```

```python
import jax
import jax.numpy as jnp
from jax import lax
from jax.sharding import Mesh, PartitionSpec as P

HDIM = 64
SEG_MAX = 1020


negative_fill = -1e30
epsilon = 1e-05


def layer_norm(matrix):
    values = matrix.astype(jnp.float32)
    average = jnp.mean(values, axis=-1, keepdims=True)
    centred = values - average
    variance = jnp.mean(centred * centred, axis=-1, keepdims=True)
    return (centred * lax.rsqrt(variance + epsilon)).astype(jnp.bfloat16)


def softmax_part(scores, visible, values, pattern):
    top = jnp.max(jnp.where(visible, scores, negative_fill), axis=-1)
    weights = jnp.where(visible, jnp.exp(scores - top[..., None]), 0.0)
    total = jnp.sum(weights, axis=-1)
    output = jnp.einsum(
        pattern, weights.astype(jnp.bfloat16), values, preferred_element_type=jnp.float32
    )
    return (top, total, output)


def combine_parts(first, second):
    top = jnp.maximum(first[0], second[0])
    scale_one = jnp.exp(first[0] - top)
    scale_two = jnp.exp(second[0] - top)
    return (
        top,
        first[1] * scale_one + second[1] * scale_two,
        first[2] * scale_one[..., None] + second[2] * scale_two[..., None],
    )


def block_rows(queries, heads):
    count, width = queries.shape
    rep = jnp.repeat(queries, heads, axis=0)
    row_head = jnp.arange(count * heads, dtype=jnp.int32) % heads
    col_head = jnp.arange(width, dtype=jnp.int32) // HDIM
    return jnp.where(row_head[:, None] == col_head[None, :], rep, jnp.zeros_like(rep))


def take_heads(output, count, heads):
    split = output.reshape(count, heads, heads, HDIM)
    eye = jnp.arange(heads)[:, None] == jnp.arange(heads)[None, :]
    return jnp.sum(jnp.where(eye[None, :, :, None], split, 0.0), axis=2)


def flat_part(query_rows, keys, values, visible, scale):
    scores = (
        lax.dot_general(
            keys, query_rows, (((1,), (1,)), ((), ())), preferred_element_type=jnp.float32
        )
        * scale
    )
    top = jnp.max(jnp.where(visible, scores, negative_fill), axis=0)
    weights = jnp.where(visible, jnp.exp(scores - top[None, :]), 0.0)
    total = jnp.sum(weights, axis=0)
    output = jnp.dot(weights.T.astype(jnp.bfloat16), values, preferred_element_type=jnp.float32)
    return top, total, output


def page_slots(table, page_ids):
    matches = table[:, None] == page_ids[None, :]
    index = jnp.arange(table.shape[0], dtype=jnp.int32)
    return jnp.sum(jnp.where(matches, index[:, None], 0), axis=0)


def ring(axis, shift):
    size = lax.axis_size(axis)
    return [(i, (i + shift) % size) for i in range(size)]


def gather_any(rows):
    chips = lax.axis_size("tx")
    held = jnp.stack(
        [rows] + [lax.ppermute(rows, "tx", ring("tx", k)) for k in range(1, chips)]
    )
    return jnp.stack([held, lax.ppermute(held, "tc", ring("tc", 1))])


def block_order():
    chips = lax.axis_size("tx")
    chip = lax.axis_index("tx")
    core = lax.axis_index("tc")
    step = jnp.arange(chips, dtype=jnp.int32)
    side = jnp.arange(2, dtype=jnp.int32)
    return (((chip - step) % chips)[None, :] * 2 + (core ^ side)[:, None]).reshape(-1)


def gather_split(rows):
    chips = lax.axis_size("tx")
    own = jnp.stack([rows, lax.ppermute(rows, "tc", ring("tc", 1))])
    entries = [own]
    for k in range(1, chips):
        far = lax.ppermute(rows, "tx", ring("tx", k))
        entries.append(jnp.stack([far, lax.ppermute(far, "tc", ring("tc", 1))]))
    return entries


def scatter_split(parts):
    chips = len(parts)
    total = None
    for k in range(chips):
        chip_sum = parts[k][0].astype(jnp.float32) + lax.ppermute(
            parts[k][1], "tc", ring("tc", 1)
        ).astype(jnp.float32)
        if k == 0:
            total = chip_sum if total is None else total + chip_sum
        else:
            moved = lax.ppermute(chip_sum.astype(jnp.bfloat16), "tx", ring("tx", chips - k))
            total = moved.astype(jnp.float32) if total is None else total + moved.astype(jnp.float32)
    return total


def scatter_any(partial):
    chips = lax.axis_size("tx")
    chip_sum = partial[0].astype(jnp.float32) + lax.ppermute(
        partial[1], "tc", ring("tc", 1)
    ).astype(jnp.float32)
    chip_half = chip_sum.astype(jnp.bfloat16)
    total = chip_sum[0]
    for k in range(1, chips):
        total = total + lax.ppermute(chip_half[k], "tx", ring("tx", chips - k)).astype(
            jnp.float32
        )
    return total


def per_device(
    tokens,
    w_qkv,
    w_out,
    w_up,
    w_down,
    key_pool,
    value_pool,
    prefix_keys,
    prefix_values,
    page_table,
    own_len,
    group_of,
    prefix_table,
    prefix_len,
    seg_ids,
):
    chips = lax.axis_size("tx")
    cores = lax.axis_size("tc")
    tensor_size = chips * cores
    data_rank = lax.axis_index("dp")
    local_rows = tokens.shape[0]
    group_len = local_rows * tensor_size
    decodes = own_len.shape[1]
    prefill = group_len - decodes
    width = w_out.shape[0]
    heads_local = width // HDIM
    scale = HDIM ** (-0.5)
    pieces = gather_any(layer_norm(tokens)).reshape(tensor_size, local_rows, -1)
    qkv = jnp.einsum(
        "jtd,kde->kjte", pieces, w_qkv, preferred_element_type=jnp.float32
    ).astype(jnp.bfloat16)
    order = block_order()
    inverse = jnp.argsort(order)

    def block_of(kind, index):
        return lax.dynamic_index_in_dim(qkv[kind], inverse[index], 0, keepdims=False)

    labels = jnp.concatenate([seg_ids[0], -1 - jnp.arange(decodes, dtype=jnp.int32)])

    block = local_rows
    tops, totals, outs = [], [], []
    for index in range(tensor_size):
        first = index * block
        low_block = max(0, (first - (SEG_MAX - 1)) // block)
        low = low_block * block
        high = first + block
        span = high - low
        query_block = block_of(0, index).reshape(block, heads_local, HDIM)
        key_block = jnp.concatenate(
            [block_of(1, b) for b in range(low_block, index + 1)], axis=0
        ).reshape(span, heads_local, HDIM)
        value_block = jnp.concatenate(
            [block_of(2, b) for b in range(low_block, index + 1)], axis=0
        ).reshape(span, heads_local, HDIM)
        scores = (
            jnp.einsum("qhe,khe->hqk", query_block, key_block, preferred_element_type=jnp.float32)
            * scale
        )
        query_pos = jnp.arange(first, high, dtype=jnp.int32)
        key_pos = jnp.arange(low, high, dtype=jnp.int32)
        visible = (labels[first:high][:, None] == labels[low:high][None, :]) & (
            key_pos[None, :] <= query_pos[:, None]
        )
        part = softmax_part(scores, visible[None, :, :], value_block, "hqk,khe->qhe")
        tops.append(part[0].T)
        totals.append(part[1].T)
        outs.append(part[2])
    top = jnp.concatenate(tops, axis=0)
    total = jnp.concatenate(totals, axis=0)
    output = jnp.concatenate(outs, axis=0)

    dec_queries = block_of(0, tensor_size - 1)[local_rows - decodes :]
    rows_h = decodes * heads_local
    row_req = jnp.arange(rows_h, dtype=jnp.int32) // heads_local

    pages, page_len = key_pool.shape[0], key_pool.shape[1]
    table = page_table[0]
    own_pages = table.shape[0] // decodes
    slot = page_slots(table, jnp.arange(pages, dtype=jnp.int32))
    owner = jnp.repeat(slot // own_pages, page_len)
    offset = ((slot % own_pages)[:, None] * page_len + jnp.arange(page_len)[None, :]).reshape(-1)
    own_visible = (owner[:, None] == row_req[None, :]) & (
        offset[:, None] < own_len[0][row_req][None, :]
    )
    o_top, o_total, o_out = flat_part(
        block_rows(dec_queries, heads_local),
        key_pool.reshape(pages * page_len, width),
        value_pool.reshape(pages * page_len, width),
        own_visible,
        scale,
    )
    own_part = (
        o_top.reshape(decodes, heads_local),
        o_total.reshape(decodes, heads_local),
        take_heads(o_out, decodes, heads_local),
    )

    data_size = lax.axis_size("dp")
    shifted = [dec_queries] + [
        lax.ppermute(dec_queries, "dp", [(i, (i + k) % data_size) for i in range(data_size)])
        for k in range(1, data_size)
    ]
    source_order = (data_rank - jnp.arange(data_size, dtype=jnp.int32)) % data_size
    all_queries = jnp.take(jnp.stack(shifted), source_order, axis=0).reshape(
        data_size * decodes, width
    )
    all_count = all_queries.shape[0]
    all_rows = all_count * heads_local
    pre_local = prefix_keys.shape[0]
    per_prefix = prefix_table.shape[0] // prefix_len.shape[0]
    page_ids = data_rank * pre_local + jnp.arange(pre_local, dtype=jnp.int32)
    pslot = page_slots(prefix_table, page_ids)
    p_owner = jnp.repeat(pslot // per_prefix, page_len)
    p_offset = (
        (pslot % per_prefix)[:, None] * page_len + jnp.arange(page_len)[None, :]
    ).reshape(-1)
    row_prefix = group_of.reshape(-1)[jnp.arange(all_rows, dtype=jnp.int32) // heads_local]
    p_visible = (p_owner[:, None] == row_prefix[None, :]) & (
        p_offset[:, None] < prefix_len[row_prefix][None, :]
    )
    p_top, p_total, p_out = flat_part(
        block_rows(all_queries, heads_local),
        prefix_keys.reshape(pre_local * page_len, width),
        prefix_values.reshape(pre_local * page_len, width),
        p_visible,
        scale,
    )
    packed = jnp.concatenate(
        [
            take_heads(p_out, all_count, heads_local),
            p_top.reshape(all_count, heads_local, 1),
            p_total.reshape(all_count, heads_local, 1),
        ],
        axis=-1,
    )
    received = [lax.dynamic_slice_in_dim(packed, data_rank * decodes, decodes, axis=0)]
    for k in range(1, data_size):
        target = (data_rank + k) % data_size
        outgoing = lax.dynamic_slice_in_dim(packed, target * decodes, decodes, axis=0)
        received.append(
            lax.ppermute(outgoing, "dp", [(i, (i + k) % data_size) for i in range(data_size)])
        )
    mine = jnp.stack(received)
    m_all = mine[..., HDIM]
    p_max = jnp.max(m_all, axis=0)
    p_scale = jnp.exp(m_all - p_max[None])
    prefix_result = (
        p_max,
        jnp.sum(mine[..., HDIM + 1] * p_scale, axis=0),
        jnp.sum(mine[..., :HDIM] * p_scale[..., None], axis=0),
    )

    batch_dec = (top[prefill:], total[prefill:], output[prefill:])
    merged_dec = combine_parts(combine_parts(batch_dec, own_part), prefix_result)
    total = jnp.concatenate([total[:prefill], merged_dec[1]], axis=0)
    output = jnp.concatenate([output[:prefill], merged_dec[2]], axis=0)
    attention = (output / total[..., None]).reshape(group_len, width).astype(jnp.bfloat16)
    projected = jnp.stack(
        [
            jnp.dot(
                lax.dynamic_slice_in_dim(attention, order[j] * local_rows, local_rows, 0),
                w_out,
                preferred_element_type=jnp.float32,
            ).astype(jnp.bfloat16)
            for j in range(tensor_size)
        ]
    )
    state = (
        tokens.astype(jnp.float32)
        + scatter_any(projected.reshape(2, chips, local_rows, -1))
    ).astype(jnp.bfloat16)
    mlp_parts = []
    for state_rows in gather_split(layer_norm(state)):
        hidden = jax.nn.gelu(
            jnp.einsum("srd,df->srf", state_rows, w_up, preferred_element_type=jnp.float32),
            approximate=False,
        ).astype(jnp.bfloat16)
        mlp_parts.append(
            jnp.einsum(
                "srf,fd->srd", hidden, w_down, preferred_element_type=jnp.float32
            ).astype(jnp.bfloat16)
        )
    mlp_share = scatter_split(mlp_parts)
    return (state.astype(jnp.float32) + mlp_share).astype(jnp.bfloat16)


def solution(mesh):
    data_size = mesh.shape["dp"]
    tensor_size = mesh.shape["tensor"]
    split = Mesh(mesh.devices.reshape(data_size, tensor_size // 2, 2), ("dp", "tx", "tc"))
    placed = (
        P(("dp", "tx", "tc"), None),
        P(None, None, ("tx", "tc")),
        P(("tx", "tc"), None),
        P(None, ("tx", "tc")),
        P(("tx", "tc"), None),
        P("dp", None, ("tx", "tc")),
        P("dp", None, ("tx", "tc")),
        P("dp", None, ("tx", "tc")),
        P("dp", None, ("tx", "tc")),
        P("dp", None),
        P("dp", None),
        P(),
        P(),
        P(),
        P("dp", None),
    )

    return jax.shard_map(
        per_device, mesh=split, in_specs=placed, out_specs=P(("dp", "tx", "tc"), None), check_vma=False
    )
```

```python
import jax
import jax.numpy as jnp
from jax import lax
from jax.sharding import Mesh, PartitionSpec as P

HDIM = 64
SEG_MAX = 1020


negative_fill = -1e30
epsilon = 1e-05


def layer_norm(matrix):
    values = matrix.astype(jnp.float32)
    average = jnp.mean(values, axis=-1, keepdims=True)
    centred = values - average
    variance = jnp.mean(centred * centred, axis=-1, keepdims=True)
    return (centred * lax.rsqrt(variance + epsilon)).astype(jnp.bfloat16)


def softmax_part(scores, visible, values, pattern):
    top = jnp.max(jnp.where(visible, scores, negative_fill), axis=-1)
    weights = jnp.where(visible, jnp.exp(scores - top[..., None]), 0.0)
    total = jnp.sum(weights, axis=-1)
    output = jnp.einsum(
        pattern, weights.astype(jnp.bfloat16), values, preferred_element_type=jnp.float32
    )
    return (top, total, output)


def combine_parts(first, second):
    top = jnp.maximum(first[0], second[0])
    scale_one = jnp.exp(first[0] - top)
    scale_two = jnp.exp(second[0] - top)
    return (
        top,
        first[1] * scale_one + second[1] * scale_two,
        first[2] * scale_one[..., None] + second[2] * scale_two[..., None],
    )


def block_rows(queries, heads):
    count, width = queries.shape
    rep = jnp.repeat(queries, heads, axis=0)
    row_head = jnp.arange(count * heads, dtype=jnp.int32) % heads
    col_head = jnp.arange(width, dtype=jnp.int32) // HDIM
    return jnp.where(row_head[:, None] == col_head[None, :], rep, jnp.zeros_like(rep))


def take_heads(output, count, heads):
    split = output.reshape(count, heads, heads, HDIM)
    eye = jnp.arange(heads)[:, None] == jnp.arange(heads)[None, :]
    return jnp.sum(jnp.where(eye[None, :, :, None], split, 0.0), axis=2)


def flat_part(query_rows, keys, values, visible, scale):
    scores = (
        lax.dot_general(
            keys, query_rows, (((1,), (1,)), ((), ())), preferred_element_type=jnp.float32
        )
        * scale
    )
    top = jnp.max(jnp.where(visible, scores, negative_fill), axis=0)
    weights = jnp.where(visible, jnp.exp(scores - top[None, :]), 0.0)
    total = jnp.sum(weights, axis=0)
    output = jnp.dot(weights.T.astype(jnp.bfloat16), values, preferred_element_type=jnp.float32)
    return top, total, output


def page_slots(table, page_ids):
    matches = table[:, None] == page_ids[None, :]
    index = jnp.arange(table.shape[0], dtype=jnp.int32)
    return jnp.sum(jnp.where(matches, index[:, None], 0), axis=0)


def ring(axis, shift):
    size = lax.axis_size(axis)
    return [(i, (i + shift) % size) for i in range(size)]


def gather_any(rows):
    chips = lax.axis_size("tx")
    held = jnp.stack(
        [rows] + [lax.ppermute(rows, "tx", ring("tx", k)) for k in range(1, chips)]
    )
    return jnp.stack([held, lax.ppermute(held, "tc", ring("tc", 1))])


def block_order():
    chips = lax.axis_size("tx")
    chip = lax.axis_index("tx")
    core = lax.axis_index("tc")
    step = jnp.arange(chips, dtype=jnp.int32)
    side = jnp.arange(2, dtype=jnp.int32)
    return (((chip - step) % chips)[None, :] * 2 + (core ^ side)[:, None]).reshape(-1)


def gather_split(rows):
    chips = lax.axis_size("tx")
    own = jnp.stack([rows, lax.ppermute(rows, "tc", ring("tc", 1))])
    entries = [own]
    for k in range(1, chips):
        far = lax.ppermute(rows, "tx", ring("tx", k))
        entries.append(jnp.stack([far, lax.ppermute(far, "tc", ring("tc", 1))]))
    return entries


def scatter_split(parts):
    chips = len(parts)

    def chip_sum(part):
        return part[0].astype(jnp.float32) + lax.ppermute(part[1], "tc", ring("tc", 1)).astype(
            jnp.float32
        )

    total = chip_sum(parts[0])
    pieces = []
    for h in range(len(parts[1]) if chips > 1 else 0):
        piece = None
        for k in range(1, chips):
            moved = lax.ppermute(
                chip_sum(parts[k][h]).astype(jnp.bfloat16), "tx", ring("tx", chips - k)
            ).astype(jnp.float32)
            piece = moved if piece is None else piece + moved
        pieces.append(piece)
    if pieces:
        total = total + jnp.concatenate(pieces, axis=0)
    return total


def scatter_any(partial):
    chips = lax.axis_size("tx")
    chip_sum = partial[0].astype(jnp.float32) + lax.ppermute(
        partial[1], "tc", ring("tc", 1)
    ).astype(jnp.float32)
    chip_half = chip_sum.astype(jnp.bfloat16)
    total = chip_sum[0]
    for k in range(1, chips):
        total = total + lax.ppermute(chip_half[k], "tx", ring("tx", chips - k)).astype(
            jnp.float32
        )
    return total


def per_device(
    tokens,
    w_qkv,
    w_out,
    w_up,
    w_down,
    key_pool,
    value_pool,
    prefix_keys,
    prefix_values,
    page_table,
    own_len,
    group_of,
    prefix_table,
    prefix_len,
    seg_ids,
):
    chips = lax.axis_size("tx")
    cores = lax.axis_size("tc")
    tensor_size = chips * cores
    data_rank = lax.axis_index("dp")
    local_rows = tokens.shape[0]
    group_len = local_rows * tensor_size
    decodes = own_len.shape[1]
    prefill = group_len - decodes
    width = w_out.shape[0]
    heads_local = width // HDIM
    scale = HDIM ** (-0.5)
    pieces = gather_any(layer_norm(tokens)).reshape(tensor_size, local_rows, -1)
    qkv = jnp.einsum(
        "jtd,kde->kjte", pieces, w_qkv, preferred_element_type=jnp.float32
    ).astype(jnp.bfloat16)
    order = block_order()
    inverse = jnp.argsort(order)

    def block_of(kind, index):
        return lax.dynamic_index_in_dim(qkv[kind], inverse[index], 0, keepdims=False)

    labels = jnp.concatenate([seg_ids[0], -1 - jnp.arange(decodes, dtype=jnp.int32)])

    block = local_rows
    tops, totals, outs = [], [], []
    for index in range(tensor_size):
        first = index * block
        low_block = max(0, (first - (SEG_MAX - 1)) // block)
        low = low_block * block
        high = first + block
        span = high - low
        query_block = block_of(0, index).reshape(block, heads_local, HDIM)
        key_block = jnp.concatenate(
            [block_of(1, b) for b in range(low_block, index + 1)], axis=0
        ).reshape(span, heads_local, HDIM)
        value_block = jnp.concatenate(
            [block_of(2, b) for b in range(low_block, index + 1)], axis=0
        ).reshape(span, heads_local, HDIM)
        scores = (
            jnp.einsum("qhe,khe->hqk", query_block, key_block, preferred_element_type=jnp.float32)
            * scale
        )
        query_pos = jnp.arange(first, high, dtype=jnp.int32)
        key_pos = jnp.arange(low, high, dtype=jnp.int32)
        visible = (labels[first:high][:, None] == labels[low:high][None, :]) & (
            key_pos[None, :] <= query_pos[:, None]
        )
        part = softmax_part(scores, visible[None, :, :], value_block, "hqk,khe->qhe")
        tops.append(part[0].T)
        totals.append(part[1].T)
        outs.append(part[2])
    top = jnp.concatenate(tops, axis=0)
    total = jnp.concatenate(totals, axis=0)
    output = jnp.concatenate(outs, axis=0)

    dec_queries = block_of(0, tensor_size - 1)[local_rows - decodes :]
    rows_h = decodes * heads_local
    row_req = jnp.arange(rows_h, dtype=jnp.int32) // heads_local

    pages, page_len = key_pool.shape[0], key_pool.shape[1]
    table = page_table[0]
    own_pages = table.shape[0] // decodes
    slot = page_slots(table, jnp.arange(pages, dtype=jnp.int32))
    owner = jnp.repeat(slot // own_pages, page_len)
    offset = ((slot % own_pages)[:, None] * page_len + jnp.arange(page_len)[None, :]).reshape(-1)
    own_visible = (owner[:, None] == row_req[None, :]) & (
        offset[:, None] < own_len[0][row_req][None, :]
    )
    o_top, o_total, o_out = flat_part(
        block_rows(dec_queries, heads_local),
        key_pool.reshape(pages * page_len, width),
        value_pool.reshape(pages * page_len, width),
        own_visible,
        scale,
    )
    own_part = (
        o_top.reshape(decodes, heads_local),
        o_total.reshape(decodes, heads_local),
        take_heads(o_out, decodes, heads_local),
    )

    data_size = lax.axis_size("dp")
    shifted = [dec_queries] + [
        lax.ppermute(dec_queries, "dp", [(i, (i + k) % data_size) for i in range(data_size)])
        for k in range(1, data_size)
    ]
    source_order = (data_rank - jnp.arange(data_size, dtype=jnp.int32)) % data_size
    all_queries = jnp.take(jnp.stack(shifted), source_order, axis=0).reshape(
        data_size * decodes, width
    )
    all_count = all_queries.shape[0]
    all_rows = all_count * heads_local
    pre_local = prefix_keys.shape[0]
    per_prefix = prefix_table.shape[0] // prefix_len.shape[0]
    page_ids = data_rank * pre_local + jnp.arange(pre_local, dtype=jnp.int32)
    pslot = page_slots(prefix_table, page_ids)
    p_owner = jnp.repeat(pslot // per_prefix, page_len)
    p_offset = (
        (pslot % per_prefix)[:, None] * page_len + jnp.arange(page_len)[None, :]
    ).reshape(-1)
    row_prefix = group_of.reshape(-1)[jnp.arange(all_rows, dtype=jnp.int32) // heads_local]
    p_visible = (p_owner[:, None] == row_prefix[None, :]) & (
        p_offset[:, None] < prefix_len[row_prefix][None, :]
    )
    p_top, p_total, p_out = flat_part(
        block_rows(all_queries, heads_local),
        prefix_keys.reshape(pre_local * page_len, width),
        prefix_values.reshape(pre_local * page_len, width),
        p_visible,
        scale,
    )
    packed = jnp.concatenate(
        [
            take_heads(p_out, all_count, heads_local),
            p_top.reshape(all_count, heads_local, 1),
            p_total.reshape(all_count, heads_local, 1),
        ],
        axis=-1,
    )
    received = [lax.dynamic_slice_in_dim(packed, data_rank * decodes, decodes, axis=0)]
    for k in range(1, data_size):
        target = (data_rank + k) % data_size
        outgoing = lax.dynamic_slice_in_dim(packed, target * decodes, decodes, axis=0)
        received.append(
            lax.ppermute(outgoing, "dp", [(i, (i + k) % data_size) for i in range(data_size)])
        )
    mine = jnp.stack(received)
    m_all = mine[..., HDIM]
    p_max = jnp.max(m_all, axis=0)
    p_scale = jnp.exp(m_all - p_max[None])
    prefix_result = (
        p_max,
        jnp.sum(mine[..., HDIM + 1] * p_scale, axis=0),
        jnp.sum(mine[..., :HDIM] * p_scale[..., None], axis=0),
    )

    batch_dec = (top[prefill:], total[prefill:], output[prefill:])
    merged_dec = combine_parts(combine_parts(batch_dec, own_part), prefix_result)
    total = jnp.concatenate([total[:prefill], merged_dec[1]], axis=0)
    output = jnp.concatenate([output[:prefill], merged_dec[2]], axis=0)
    attention = (output / total[..., None]).reshape(group_len, width).astype(jnp.bfloat16)
    projected = jnp.stack(
        [
            jnp.dot(
                lax.dynamic_slice_in_dim(attention, order[j] * local_rows, local_rows, 0),
                w_out,
                preferred_element_type=jnp.float32,
            ).astype(jnp.bfloat16)
            for j in range(tensor_size)
        ]
    )
    state = (
        tokens.astype(jnp.float32)
        + scatter_any(projected.reshape(2, chips, local_rows, -1))
    ).astype(jnp.bfloat16)

    def mlp(state_rows):
        hidden = jax.nn.gelu(
            jnp.einsum("srd,df->srf", state_rows, w_up, preferred_element_type=jnp.float32),
            approximate=False,
        ).astype(jnp.bfloat16)
        return jnp.einsum(
            "srf,fd->srd", hidden, w_down, preferred_element_type=jnp.float32
        ).astype(jnp.bfloat16)

    mlp_parts = []
    half = local_rows // 2
    for k, state_rows in enumerate(gather_split(layer_norm(state))):
        if k == 0:
            mlp_parts.append(mlp(state_rows))
        else:
            split_parts = []
            for h in range(2):
                split_parts.append(mlp(state_rows[:, h * half : (h + 1) * half]))
            mlp_parts.append(split_parts)
    mlp_share = scatter_split(mlp_parts)
    return (state.astype(jnp.float32) + mlp_share).astype(jnp.bfloat16)


def solution(mesh):
    data_size = mesh.shape["dp"]
    tensor_size = mesh.shape["tensor"]
    split = Mesh(mesh.devices.reshape(data_size, tensor_size // 2, 2), ("dp", "tx", "tc"))
    placed = (
        P(("dp", "tx", "tc"), None),
        P(None, None, ("tx", "tc")),
        P(("tx", "tc"), None),
        P(None, ("tx", "tc")),
        P(("tx", "tc"), None),
        P("dp", None, ("tx", "tc")),
        P("dp", None, ("tx", "tc")),
        P("dp", None, ("tx", "tc")),
        P("dp", None, ("tx", "tc")),
        P("dp", None),
        P("dp", None),
        P(),
        P(),
        P(),
        P("dp", None),
    )

    return jax.shard_map(
        per_device, mesh=split, in_specs=placed, out_specs=P(("dp", "tx", "tc"), None), check_vma=False
    )
```

```python
import jax
import jax.numpy as jnp
from jax import lax
from jax.sharding import Mesh, PartitionSpec as P

HDIM = 64
SEG_MAX = 1020


negative_fill = -1e30
epsilon = 1e-05


def layer_norm(matrix):
    values = matrix.astype(jnp.float32)
    average = jnp.mean(values, axis=-1, keepdims=True)
    centred = values - average
    variance = jnp.mean(centred * centred, axis=-1, keepdims=True)
    return (centred * lax.rsqrt(variance + epsilon)).astype(jnp.bfloat16)


def softmax_part(scores, visible, values, pattern):
    top = jnp.max(jnp.where(visible, scores, negative_fill), axis=-1)
    weights = jnp.where(visible, jnp.exp(scores - top[..., None]), 0.0)
    total = jnp.sum(weights, axis=-1)
    output = jnp.einsum(
        pattern, weights.astype(jnp.bfloat16), values, preferred_element_type=jnp.float32
    )
    return (top, total, output)


def combine_parts(first, second):
    top = jnp.maximum(first[0], second[0])
    scale_one = jnp.exp(first[0] - top)
    scale_two = jnp.exp(second[0] - top)
    return (
        top,
        first[1] * scale_one + second[1] * scale_two,
        first[2] * scale_one[..., None] + second[2] * scale_two[..., None],
    )


def block_rows(queries, heads):
    count, width = queries.shape
    rep = jnp.repeat(queries, heads, axis=0)
    row_head = jnp.arange(count * heads, dtype=jnp.int32) % heads
    col_head = jnp.arange(width, dtype=jnp.int32) // HDIM
    return jnp.where(row_head[:, None] == col_head[None, :], rep, jnp.zeros_like(rep))


def take_heads(output, count, heads):
    split = output.reshape(count, heads, heads, HDIM)
    eye = jnp.arange(heads)[:, None] == jnp.arange(heads)[None, :]
    return jnp.sum(jnp.where(eye[None, :, :, None], split, 0.0), axis=2)


def flat_part(query_rows, keys, values, visible, scale):
    scores = (
        lax.dot_general(
            keys, query_rows, (((1,), (1,)), ((), ())), preferred_element_type=jnp.float32
        )
        * scale
    )
    top = jnp.max(jnp.where(visible, scores, negative_fill), axis=0)
    weights = jnp.where(visible, jnp.exp(scores - top[None, :]), 0.0)
    total = jnp.sum(weights, axis=0)
    output = jnp.dot(weights.T.astype(jnp.bfloat16), values, preferred_element_type=jnp.float32)
    return top, total, output


def page_slots(table, page_ids):
    matches = table[:, None] == page_ids[None, :]
    index = jnp.arange(table.shape[0], dtype=jnp.int32)
    return jnp.sum(jnp.where(matches, index[:, None], 0), axis=0)


def ring(axis, shift):
    size = lax.axis_size(axis)
    return [(i, (i + shift) % size) for i in range(size)]


def gather_any(rows):
    chips = lax.axis_size("tx")
    held = jnp.stack(
        [rows] + [lax.ppermute(rows, "tx", ring("tx", k)) for k in range(1, chips)]
    )
    return jnp.stack([held, lax.ppermute(held, "tc", ring("tc", 1))])


def block_order():
    chips = lax.axis_size("tx")
    chip = lax.axis_index("tx")
    core = lax.axis_index("tc")
    step = jnp.arange(chips, dtype=jnp.int32)
    side = jnp.arange(2, dtype=jnp.int32)
    return (((chip - step) % chips)[None, :] * 2 + (core ^ side)[:, None]).reshape(-1)


def gather_split(rows):
    chips = lax.axis_size("tx")
    own = jnp.stack([rows, lax.ppermute(rows, "tc", ring("tc", 1))])
    entries = [own]
    for k in range(1, chips):
        far = lax.ppermute(rows, "tx", ring("tx", k))
        entries.append(jnp.stack([far, lax.ppermute(far, "tc", ring("tc", 1))]))
    return entries


def scatter_split(parts):
    chips = len(parts)

    def chip_sum(part):
        return part[0].astype(jnp.float32) + lax.ppermute(part[1], "tc", ring("tc", 1)).astype(
            jnp.float32
        )

    total = chip_sum(parts[0])
    pieces = []
    for h in range(len(parts[1]) if chips > 1 else 0):
        piece = None
        for k in range(1, chips):
            outgoing = chip_sum(parts[k][h]).astype(jnp.bfloat16)
            moved = lax.ppermute(outgoing, "tx", ring("tx", chips - k)).astype(jnp.float32)
            piece = moved if piece is None else piece + moved
        pieces.append(piece)
    if pieces:
        total = total + jnp.concatenate(pieces, axis=0)
    return total


def scatter_any(partial):
    chips = lax.axis_size("tx")
    chip_sum = partial[0].astype(jnp.float32) + lax.ppermute(
        partial[1], "tc", ring("tc", 1)
    ).astype(jnp.float32)
    chip_half = chip_sum.astype(jnp.bfloat16)
    total = chip_sum[0]
    for k in range(1, chips):
        total = total + lax.ppermute(chip_half[k], "tx", ring("tx", chips - k)).astype(
            jnp.float32
        )
    return total


def per_device(
    tokens,
    w_qkv,
    w_out,
    w_up,
    w_down,
    key_pool,
    value_pool,
    prefix_keys,
    prefix_values,
    page_table,
    own_len,
    group_of,
    prefix_table,
    prefix_len,
    seg_ids,
):
    chips = lax.axis_size("tx")
    cores = lax.axis_size("tc")
    tensor_size = chips * cores
    data_rank = lax.axis_index("dp")
    local_rows = tokens.shape[0]
    group_len = local_rows * tensor_size
    decodes = own_len.shape[1]
    prefill = group_len - decodes
    width = w_out.shape[0]
    heads_local = width // HDIM
    scale = HDIM ** (-0.5)
    pieces = gather_any(layer_norm(tokens)).reshape(tensor_size, local_rows, -1)
    qkv = jnp.einsum(
        "jtd,kde->kjte", pieces, w_qkv, preferred_element_type=jnp.float32
    ).astype(jnp.bfloat16)
    order = block_order()
    inverse = jnp.argsort(order)

    def block_of(kind, index):
        return lax.dynamic_index_in_dim(qkv[kind], inverse[index], 0, keepdims=False)

    labels = jnp.concatenate([seg_ids[0], -1 - jnp.arange(decodes, dtype=jnp.int32)])

    block = local_rows
    tops, totals, outs = [], [], []
    for index in range(tensor_size):
        first = index * block
        low_block = max(0, (first - (SEG_MAX - 1)) // block)
        low = low_block * block
        high = first + block
        span = high - low
        query_block = block_of(0, index).reshape(block, heads_local, HDIM)
        key_block = jnp.concatenate(
            [block_of(1, b) for b in range(low_block, index + 1)], axis=0
        ).reshape(span, heads_local, HDIM)
        value_block = jnp.concatenate(
            [block_of(2, b) for b in range(low_block, index + 1)], axis=0
        ).reshape(span, heads_local, HDIM)
        scores = (
            jnp.einsum("qhe,khe->hqk", query_block, key_block, preferred_element_type=jnp.float32)
            * scale
        )
        query_pos = jnp.arange(first, high, dtype=jnp.int32)
        key_pos = jnp.arange(low, high, dtype=jnp.int32)
        visible = (labels[first:high][:, None] == labels[low:high][None, :]) & (
            key_pos[None, :] <= query_pos[:, None]
        )
        part = softmax_part(scores, visible[None, :, :], value_block, "hqk,khe->qhe")
        tops.append(part[0].T)
        totals.append(part[1].T)
        outs.append(part[2])
    top = jnp.concatenate(tops, axis=0)
    total = jnp.concatenate(totals, axis=0)
    output = jnp.concatenate(outs, axis=0)

    dec_queries = block_of(0, tensor_size - 1)[local_rows - decodes :]
    rows_h = decodes * heads_local
    row_req = jnp.arange(rows_h, dtype=jnp.int32) // heads_local

    pages, page_len = key_pool.shape[0], key_pool.shape[1]
    table = page_table[0]
    own_pages = table.shape[0] // decodes
    slot = page_slots(table, jnp.arange(pages, dtype=jnp.int32))
    owner = jnp.repeat(slot // own_pages, page_len)
    offset = ((slot % own_pages)[:, None] * page_len + jnp.arange(page_len)[None, :]).reshape(-1)
    own_visible = (owner[:, None] == row_req[None, :]) & (
        offset[:, None] < own_len[0][row_req][None, :]
    )
    o_top, o_total, o_out = flat_part(
        block_rows(dec_queries, heads_local),
        key_pool.reshape(pages * page_len, width),
        value_pool.reshape(pages * page_len, width),
        own_visible,
        scale,
    )
    own_part = (
        o_top.reshape(decodes, heads_local),
        o_total.reshape(decodes, heads_local),
        take_heads(o_out, decodes, heads_local),
    )

    data_size = lax.axis_size("dp")
    shifted = [dec_queries] + [
        lax.ppermute(dec_queries, "dp", [(i, (i + k) % data_size) for i in range(data_size)])
        for k in range(1, data_size)
    ]
    source_order = (data_rank - jnp.arange(data_size, dtype=jnp.int32)) % data_size
    all_queries = jnp.take(jnp.stack(shifted), source_order, axis=0).reshape(
        data_size * decodes, width
    )
    all_count = all_queries.shape[0]
    all_rows = all_count * heads_local
    pre_local = prefix_keys.shape[0]
    per_prefix = prefix_table.shape[0] // prefix_len.shape[0]
    page_ids = data_rank * pre_local + jnp.arange(pre_local, dtype=jnp.int32)
    pslot = page_slots(prefix_table, page_ids)
    p_owner = jnp.repeat(pslot // per_prefix, page_len)
    p_offset = (
        (pslot % per_prefix)[:, None] * page_len + jnp.arange(page_len)[None, :]
    ).reshape(-1)
    row_prefix = group_of.reshape(-1)[jnp.arange(all_rows, dtype=jnp.int32) // heads_local]
    p_visible = (p_owner[:, None] == row_prefix[None, :]) & (
        p_offset[:, None] < prefix_len[row_prefix][None, :]
    )
    p_top, p_total, p_out = flat_part(
        block_rows(all_queries, heads_local),
        prefix_keys.reshape(pre_local * page_len, width),
        prefix_values.reshape(pre_local * page_len, width),
        p_visible,
        scale,
    )
    packed = jnp.concatenate(
        [
            take_heads(p_out, all_count, heads_local),
            p_top.reshape(all_count, heads_local, 1),
            p_total.reshape(all_count, heads_local, 1),
        ],
        axis=-1,
    )
    received = [lax.dynamic_slice_in_dim(packed, data_rank * decodes, decodes, axis=0)]
    for k in range(1, data_size):
        target = (data_rank + k) % data_size
        outgoing = lax.dynamic_slice_in_dim(packed, target * decodes, decodes, axis=0)
        received.append(
            lax.ppermute(outgoing, "dp", [(i, (i + k) % data_size) for i in range(data_size)])
        )
    mine = jnp.stack(received)
    m_all = mine[..., HDIM]
    p_max = jnp.max(m_all, axis=0)
    p_scale = jnp.exp(m_all - p_max[None])
    prefix_result = (
        p_max,
        jnp.sum(mine[..., HDIM + 1] * p_scale, axis=0),
        jnp.sum(mine[..., :HDIM] * p_scale[..., None], axis=0),
    )

    batch_dec = (top[prefill:], total[prefill:], output[prefill:])
    merged_dec = combine_parts(combine_parts(batch_dec, own_part), prefix_result)
    total = jnp.concatenate([total[:prefill], merged_dec[1]], axis=0)
    output = jnp.concatenate([output[:prefill], merged_dec[2]], axis=0)
    attention = (output / total[..., None]).reshape(group_len, width).astype(jnp.bfloat16)
    projected = jnp.stack(
        [
            jnp.dot(
                lax.dynamic_slice_in_dim(attention, order[j] * local_rows, local_rows, 0),
                w_out,
                preferred_element_type=jnp.float32,
            ).astype(jnp.bfloat16)
            for j in range(tensor_size)
        ]
    )
    state = (
        tokens.astype(jnp.float32)
        + scatter_any(projected.reshape(2, chips, local_rows, -1))
    ).astype(jnp.bfloat16)

    def mlp(state_rows):
        hidden = jax.nn.gelu(
            jnp.einsum("srd,df->srf", state_rows, w_up, preferred_element_type=jnp.float32),
            approximate=False,
        ).astype(jnp.bfloat16)
        return jnp.einsum(
            "srf,fd->srd", hidden, w_down, preferred_element_type=jnp.float32
        ).astype(jnp.bfloat16)

    mlp_parts = []
    half = local_rows // 2
    for k, state_rows in enumerate(gather_split(layer_norm(state))):
        if k == 0:
            mlp_parts.append(mlp(state_rows))
        else:
            split_parts = []
            for h in range(2):
                split_parts.append(mlp(state_rows[:, h * half : (h + 1) * half]))
            mlp_parts.append(split_parts)
    mlp_share = scatter_split(mlp_parts)
    return (state.astype(jnp.float32) + mlp_share).astype(jnp.bfloat16)


def solution(mesh):
    data_size = mesh.shape["dp"]
    tensor_size = mesh.shape["tensor"]
    split = Mesh(mesh.devices.reshape(data_size, tensor_size // 2, 2), ("dp", "tx", "tc"))
    placed = (
        P(("dp", "tx", "tc"), None),
        P(None, None, ("tx", "tc")),
        P(("tx", "tc"), None),
        P(None, ("tx", "tc")),
        P(("tx", "tc"), None),
        P("dp", None, ("tx", "tc")),
        P("dp", None, ("tx", "tc")),
        P("dp", None, ("tx", "tc")),
        P("dp", None, ("tx", "tc")),
        P("dp", None),
        P("dp", None),
        P(),
        P(),
        P(),
        P("dp", None),
    )

    return jax.shard_map(
        per_device, mesh=split, in_specs=placed, out_specs=P(("dp", "tx", "tc"), None), check_vma=False
    )
```

```python
import jax
import jax.numpy as jnp
from jax import lax
from jax.sharding import Mesh, PartitionSpec as P

HDIM = 64
SEG_MAX = 1020
FAR_PIECES = 4


negative_fill = -1e30
epsilon = 1e-05


def layer_norm(matrix):
    values = matrix.astype(jnp.float32)
    average = jnp.mean(values, axis=-1, keepdims=True)
    centred = values - average
    variance = jnp.mean(centred * centred, axis=-1, keepdims=True)
    return (centred * lax.rsqrt(variance + epsilon)).astype(jnp.bfloat16)


def softmax_part(scores, visible, values, pattern):
    top = jnp.max(jnp.where(visible, scores, negative_fill), axis=-1)
    weights = jnp.where(visible, jnp.exp(scores - top[..., None]), 0.0)
    total = jnp.sum(weights, axis=-1)
    output = jnp.einsum(
        pattern, weights.astype(jnp.bfloat16), values, preferred_element_type=jnp.float32
    )
    return (top, total, output)


def combine_parts(first, second):
    top = jnp.maximum(first[0], second[0])
    scale_one = jnp.exp(first[0] - top)
    scale_two = jnp.exp(second[0] - top)
    return (
        top,
        first[1] * scale_one + second[1] * scale_two,
        first[2] * scale_one[..., None] + second[2] * scale_two[..., None],
    )


def block_rows(queries, heads):
    count, width = queries.shape
    rep = jnp.repeat(queries, heads, axis=0)
    row_head = jnp.arange(count * heads, dtype=jnp.int32) % heads
    col_head = jnp.arange(width, dtype=jnp.int32) // HDIM
    return jnp.where(row_head[:, None] == col_head[None, :], rep, jnp.zeros_like(rep))


def take_heads(output, count, heads):
    split = output.reshape(count, heads, heads, HDIM)
    eye = jnp.arange(heads)[:, None] == jnp.arange(heads)[None, :]
    return jnp.sum(jnp.where(eye[None, :, :, None], split, 0.0), axis=2)


def flat_part(query_rows, keys, values, visible, scale):
    scores = (
        lax.dot_general(
            keys, query_rows, (((1,), (1,)), ((), ())), preferred_element_type=jnp.float32
        )
        * scale
    )
    top = jnp.max(jnp.where(visible, scores, negative_fill), axis=0)
    weights = jnp.where(visible, jnp.exp(scores - top[None, :]), 0.0)
    total = jnp.sum(weights, axis=0)
    output = jnp.dot(weights.T.astype(jnp.bfloat16), values, preferred_element_type=jnp.float32)
    return top, total, output


def page_slots(table, page_ids):
    matches = table[:, None] == page_ids[None, :]
    index = jnp.arange(table.shape[0], dtype=jnp.int32)
    return jnp.sum(jnp.where(matches, index[:, None], 0), axis=0)


def ring(axis, shift):
    size = lax.axis_size(axis)
    return [(i, (i + shift) % size) for i in range(size)]


def gather_any(rows):
    chips = lax.axis_size("tx")
    held = jnp.stack(
        [rows] + [lax.ppermute(rows, "tx", ring("tx", k)) for k in range(1, chips)]
    )
    return jnp.stack([held, lax.ppermute(held, "tc", ring("tc", 1))])


def block_order():
    chips = lax.axis_size("tx")
    chip = lax.axis_index("tx")
    core = lax.axis_index("tc")
    step = jnp.arange(chips, dtype=jnp.int32)
    side = jnp.arange(2, dtype=jnp.int32)
    return (((chip - step) % chips)[None, :] * 2 + (core ^ side)[:, None]).reshape(-1)


def gather_split(rows):
    chips = lax.axis_size("tx")
    own = jnp.stack([rows, lax.ppermute(rows, "tc", ring("tc", 1))])
    entries = [own]
    for k in range(1, chips):
        far = lax.ppermute(rows, "tx", ring("tx", k))
        entries.append(jnp.stack([far, lax.ppermute(far, "tc", ring("tc", 1))]))
    return entries


def scatter_split(parts):
    chips = len(parts)

    def chip_sum(part):
        return part[0].astype(jnp.float32) + lax.ppermute(part[1], "tc", ring("tc", 1)).astype(
            jnp.float32
        )

    total = chip_sum(parts[0])
    pieces = []
    for h in range(len(parts[1]) if chips > 1 else 0):
        piece = None
        for k in range(1, chips):
            outgoing = chip_sum(parts[k][h]).astype(jnp.bfloat16)
            moved = lax.ppermute(outgoing, "tx", ring("tx", chips - k)).astype(jnp.float32)
            piece = moved if piece is None else piece + moved
        pieces.append(piece)
    if pieces:
        total = total + jnp.concatenate(pieces, axis=0)
    return total


def scatter_any(partial):
    chips = lax.axis_size("tx")
    chip_sum = partial[0].astype(jnp.float32) + lax.ppermute(
        partial[1], "tc", ring("tc", 1)
    ).astype(jnp.float32)
    chip_half = chip_sum.astype(jnp.bfloat16)
    total = chip_sum[0]
    for k in range(1, chips):
        total = total + lax.ppermute(chip_half[k], "tx", ring("tx", chips - k)).astype(
            jnp.float32
        )
    return total


def per_device(
    tokens,
    w_qkv,
    w_out,
    w_up,
    w_down,
    key_pool,
    value_pool,
    prefix_keys,
    prefix_values,
    page_table,
    own_len,
    group_of,
    prefix_table,
    prefix_len,
    seg_ids,
):
    chips = lax.axis_size("tx")
    cores = lax.axis_size("tc")
    tensor_size = chips * cores
    data_rank = lax.axis_index("dp")
    local_rows = tokens.shape[0]
    group_len = local_rows * tensor_size
    decodes = own_len.shape[1]
    prefill = group_len - decodes
    width = w_out.shape[0]
    heads_local = width // HDIM
    scale = HDIM ** (-0.5)
    pieces = gather_any(layer_norm(tokens)).reshape(tensor_size, local_rows, -1)
    qkv = jnp.einsum(
        "jtd,kde->kjte", pieces, w_qkv, preferred_element_type=jnp.float32
    ).astype(jnp.bfloat16)
    order = block_order()
    inverse = jnp.argsort(order)

    def block_of(kind, index):
        return lax.dynamic_index_in_dim(qkv[kind], inverse[index], 0, keepdims=False)

    labels = jnp.concatenate([seg_ids[0], -1 - jnp.arange(decodes, dtype=jnp.int32)])

    block = local_rows
    tops, totals, outs = [], [], []
    for index in range(tensor_size):
        first = index * block
        low_block = max(0, (first - (SEG_MAX - 1)) // block)
        low = low_block * block
        high = first + block
        span = high - low
        query_block = block_of(0, index).reshape(block, heads_local, HDIM)
        key_block = jnp.concatenate(
            [block_of(1, b) for b in range(low_block, index + 1)], axis=0
        ).reshape(span, heads_local, HDIM)
        value_block = jnp.concatenate(
            [block_of(2, b) for b in range(low_block, index + 1)], axis=0
        ).reshape(span, heads_local, HDIM)
        scores = (
            jnp.einsum("qhe,khe->hqk", query_block, key_block, preferred_element_type=jnp.float32)
            * scale
        )
        query_pos = jnp.arange(first, high, dtype=jnp.int32)
        key_pos = jnp.arange(low, high, dtype=jnp.int32)
        visible = (labels[first:high][:, None] == labels[low:high][None, :]) & (
            key_pos[None, :] <= query_pos[:, None]
        )
        part = softmax_part(scores, visible[None, :, :], value_block, "hqk,khe->qhe")
        tops.append(part[0].T)
        totals.append(part[1].T)
        outs.append(part[2])
    top = jnp.concatenate(tops, axis=0)
    total = jnp.concatenate(totals, axis=0)
    output = jnp.concatenate(outs, axis=0)

    dec_queries = block_of(0, tensor_size - 1)[local_rows - decodes :]
    rows_h = decodes * heads_local
    row_req = jnp.arange(rows_h, dtype=jnp.int32) // heads_local

    pages, page_len = key_pool.shape[0], key_pool.shape[1]
    table = page_table[0]
    own_pages = table.shape[0] // decodes
    slot = page_slots(table, jnp.arange(pages, dtype=jnp.int32))
    owner = jnp.repeat(slot // own_pages, page_len)
    offset = ((slot % own_pages)[:, None] * page_len + jnp.arange(page_len)[None, :]).reshape(-1)
    own_visible = (owner[:, None] == row_req[None, :]) & (
        offset[:, None] < own_len[0][row_req][None, :]
    )
    o_top, o_total, o_out = flat_part(
        block_rows(dec_queries, heads_local),
        key_pool.reshape(pages * page_len, width),
        value_pool.reshape(pages * page_len, width),
        own_visible,
        scale,
    )
    own_part = (
        o_top.reshape(decodes, heads_local),
        o_total.reshape(decodes, heads_local),
        take_heads(o_out, decodes, heads_local),
    )

    data_size = lax.axis_size("dp")
    shifted = [dec_queries] + [
        lax.ppermute(dec_queries, "dp", [(i, (i + k) % data_size) for i in range(data_size)])
        for k in range(1, data_size)
    ]
    source_order = (data_rank - jnp.arange(data_size, dtype=jnp.int32)) % data_size
    all_queries = jnp.take(jnp.stack(shifted), source_order, axis=0).reshape(
        data_size * decodes, width
    )
    all_count = all_queries.shape[0]
    all_rows = all_count * heads_local
    pre_local = prefix_keys.shape[0]
    per_prefix = prefix_table.shape[0] // prefix_len.shape[0]
    page_ids = data_rank * pre_local + jnp.arange(pre_local, dtype=jnp.int32)
    pslot = page_slots(prefix_table, page_ids)
    p_owner = jnp.repeat(pslot // per_prefix, page_len)
    p_offset = (
        (pslot % per_prefix)[:, None] * page_len + jnp.arange(page_len)[None, :]
    ).reshape(-1)
    row_prefix = group_of.reshape(-1)[jnp.arange(all_rows, dtype=jnp.int32) // heads_local]
    p_visible = (p_owner[:, None] == row_prefix[None, :]) & (
        p_offset[:, None] < prefix_len[row_prefix][None, :]
    )
    p_top, p_total, p_out = flat_part(
        block_rows(all_queries, heads_local),
        prefix_keys.reshape(pre_local * page_len, width),
        prefix_values.reshape(pre_local * page_len, width),
        p_visible,
        scale,
    )
    packed = jnp.concatenate(
        [
            take_heads(p_out, all_count, heads_local),
            p_top.reshape(all_count, heads_local, 1),
            p_total.reshape(all_count, heads_local, 1),
        ],
        axis=-1,
    )
    received = [lax.dynamic_slice_in_dim(packed, data_rank * decodes, decodes, axis=0)]
    for k in range(1, data_size):
        target = (data_rank + k) % data_size
        outgoing = lax.dynamic_slice_in_dim(packed, target * decodes, decodes, axis=0)
        received.append(
            lax.ppermute(outgoing, "dp", [(i, (i + k) % data_size) for i in range(data_size)])
        )
    mine = jnp.stack(received)
    m_all = mine[..., HDIM]
    p_max = jnp.max(m_all, axis=0)
    p_scale = jnp.exp(m_all - p_max[None])
    prefix_result = (
        p_max,
        jnp.sum(mine[..., HDIM + 1] * p_scale, axis=0),
        jnp.sum(mine[..., :HDIM] * p_scale[..., None], axis=0),
    )

    batch_dec = (top[prefill:], total[prefill:], output[prefill:])
    merged_dec = combine_parts(combine_parts(batch_dec, own_part), prefix_result)
    total = jnp.concatenate([total[:prefill], merged_dec[1]], axis=0)
    output = jnp.concatenate([output[:prefill], merged_dec[2]], axis=0)
    attention = (output / total[..., None]).reshape(group_len, width).astype(jnp.bfloat16)
    projected = jnp.stack(
        [
            jnp.dot(
                lax.dynamic_slice_in_dim(attention, order[j] * local_rows, local_rows, 0),
                w_out,
                preferred_element_type=jnp.float32,
            ).astype(jnp.bfloat16)
            for j in range(tensor_size)
        ]
    )
    state = (
        tokens.astype(jnp.float32)
        + scatter_any(projected.reshape(2, chips, local_rows, -1))
    ).astype(jnp.bfloat16)

    def mlp(state_rows):
        hidden = jax.nn.gelu(
            jnp.einsum("srd,df->srf", state_rows, w_up, preferred_element_type=jnp.float32),
            approximate=False,
        ).astype(jnp.bfloat16)
        return jnp.einsum(
            "srf,fd->srd", hidden, w_down, preferred_element_type=jnp.float32
        ).astype(jnp.bfloat16)

    mlp_parts = []
    piece_rows = local_rows // FAR_PIECES
    for k, state_rows in enumerate(gather_split(layer_norm(state))):
        if k == 0:
            mlp_parts.append(mlp(state_rows))
        else:
            split_parts = []
            for h in range(FAR_PIECES):
                split_parts.append(
                    mlp(state_rows[:, h * piece_rows : (h + 1) * piece_rows])
                )
            mlp_parts.append(split_parts)
    mlp_share = scatter_split(mlp_parts)
    return (state.astype(jnp.float32) + mlp_share).astype(jnp.bfloat16)


def solution(mesh):
    data_size = mesh.shape["dp"]
    tensor_size = mesh.shape["tensor"]
    split = Mesh(mesh.devices.reshape(data_size, tensor_size // 2, 2), ("dp", "tx", "tc"))
    placed = (
        P(("dp", "tx", "tc"), None),
        P(None, None, ("tx", "tc")),
        P(("tx", "tc"), None),
        P(None, ("tx", "tc")),
        P(("tx", "tc"), None),
        P("dp", None, ("tx", "tc")),
        P("dp", None, ("tx", "tc")),
        P("dp", None, ("tx", "tc")),
        P("dp", None, ("tx", "tc")),
        P("dp", None),
        P("dp", None),
        P(),
        P(),
        P(),
        P("dp", None),
    )

    return jax.shard_map(
        per_device, mesh=split, in_specs=placed, out_specs=P(("dp", "tx", "tc"), None), check_vma=False
    )
```
